32 devices in a mesh: sta: 4 (over y, x), evt: 8 (over z, core).
Axes of the slice: x: 2, y: 2, z: 4, core: 2. Of those that a mesh axis runs over, the one named last changes fastest.
Arguments:
- traces: bfloat16 [512, 96, 280], P('evt', 'sta'), may hold values from -400 to 400, as said below
- channel_valid: int32 [96], P('sta'), may hold values 0 or 1
- partner_block: int32 [512, 2], P('evt'), may hold values from 0 to 7, all different within a row; in each aligned block of 64 rows (0 to 63, 64 to 127, ...) at most 16 rows name the same one
Outputs:
- coefficient: float32 [512, 81, 128], P('evt')
The draws below stay inside these ranges and needn't reach their ends.
Inputs may be any that keep to these rules, and one draw needn't show every extreme that they name: `partner_block`: each event names 2 different blocks; among the 64 events of one block no block is named more than 16 times, and some block is named exactly 16 times. `traces`: finite trace samples.
All inputs are finite; a program needn't handle non-finite values. No bound on the sum of `channel_valid` on one device may be relied on, other than what follows from the above.
Results may differ from the reference program's by a relative error of at most 0.0003.
Values may be sent and summed in bfloat16 or wider, within the bound.
No kernel may reach another device: no remote copies, remote signals or barrier semaphores. Data moves between devices by JAX's collectives and lax.ppermute only.
A program may use at most 64 MiB of HBM per device.

```python
import math
import jax
import jax.numpy as jnp
import numpy as np
from jax import lax

CHANNELS = 96
WIN = 200
MAXLAG = 40
LAGS = 81
EXT = 280
TOP = 2
EV_DEV = 64
EVENTS = 512
CAP = 16
SLOTS = 128
N_EVT = 8


def draw_traces(key, part):
    first, second, third = jax.random.split(key, 3)
    event_scale = jnp.exp(jax.random.uniform(second, (EVENTS, 1, 1)) * math.log(10.0))
    channel_scale = jnp.exp(jax.random.uniform(third, (1, CHANNELS, 1)) * math.log(10.0))
    base = jax.random.truncated_normal(first, -4.0, 4.0, (EVENTS, CHANNELS, EXT))
    return (base * event_scale * channel_scale).astype(jnp.float32).astype(jnp.bfloat16)


def place_ends(drawn, key, least, high):
    dims = drawn.shape
    index_at = [jax.random.randint(jax.random.fold_in(key, axis), (), 0, dims[axis]) for axis in range(len(dims))]
    drawn = drawn.at[tuple(index_at)].set(least)
    longest = dims.index(max(dims))
    index_at[longest] = (index_at[longest] + 1) % dims[longest]
    return drawn.at[tuple(index_at)].set(high)


def assign_block(stream_key, own, number, rows, amount, top, bound, slope):
    order = jax.random.permutation(stream_key, amount)
    heavy_load, usual = load_shares(amount, rows * top, bound, slope, True), load_shares(amount, rows * top, bound, slope, False)
    places = jnp.arange(amount)

    def named(lengths, turn):
        used = int((lengths > 0).sum())
        fixed = max(1, used // 4)
        shifted = fixed + (places - fixed + turn * (used - fixed)) % max(1, amount - fixed)
        return jnp.zeros((amount,), jnp.int32).at[order[jnp.where(places < fixed, places, shifted)]].set(jnp.asarray(lengths, jnp.int32))

    lengths = jnp.where(number % 4 == 0, named(heavy_load, number // 4), named(usual, number - number // 4 - 1))
    mixed = jax.random.permutation(jax.random.fold_in(own, 3), amount)
    donor, receiver = mixed[0:amount // 2 * 2:2], mixed[1:amount // 2 * 2:2]
    margin = jnp.minimum(lengths[donor] - 1, bound - lengths[receiver]) // 2
    margin = jnp.where((donor == order[0]) | (receiver == order[0]) | (lengths[receiver] == 0), 0, jnp.maximum(margin, 0))
    shifted = jax.random.randint(jax.random.fold_in(own, 4), (amount // 2,), 0, 1 << 20) % (margin + 1)
    lengths = lengths.at[donor].add(-shifted).at[receiver].add(shifted)
    members = jnp.searchsorted(jnp.cumsum(lengths), jnp.arange(rows * top), side="right").astype(jnp.int32)
    grid = members.reshape(top, rows).T
    grid = grid[jax.random.permutation(jax.random.fold_in(own, 1), rows)]
    turn = jax.random.randint(jax.random.fold_in(own, 2), (rows, 1), 0, top)
    return jnp.take_along_axis(grid, (jnp.arange(top)[None, :] + turn) % top, axis=1)


def load_shares(count, total, reach, slope, full):
    loads = [(1 << 20) // math.isqrt(grade ** slope) + 1 for grade in range(1, count + 1)]
    largest = reach if full else min(reach, max(-(-total // count), total * loads[0] // sum(loads)))
    least = 1 if total - largest >= count - 1 else 0
    given, spare = [largest] + [least] * (count - 1), total - largest - least * (count - 1)
    while spare > 0:
        free = [i for i in range(1, count) if given[i] < largest] or [i for i in range(1, count) if given[i] < reach]
        mass, budget = sum([loads[i] for i in free]), spare
        for i in free:
            addition = min(reach - given[i], max(1, budget * loads[i] // mass), spare)
            given[i] = given[i] + addition
            spare = spare - addition
    return np.array(given)


def setup_inputs(seed: int = 0) -> dict:
    seeds = jax.random.split(jax.random.key(seed), 4)
    traces = draw_traces(jax.random.fold_in(seeds[3], 71), 0)
    channel_valid = place_ends((jax.random.randint(seeds[1], (CHANNELS,), 0, 4) < 3).astype(jnp.int32), jax.random.fold_in(seeds[1], 1), 0, 1)
    partner_block_keys = jax.random.split(jax.random.fold_in(seeds[2], 1), EVENTS // EV_DEV)
    partner_block_turns = jax.random.permutation(jax.random.fold_in(seeds[2], 3), EVENTS // EV_DEV)
    partner_block = jax.vmap(lambda own, number: assign_block(jax.random.fold_in(seeds[2], 2), own, number, EV_DEV, N_EVT, TOP, CAP, 2))(partner_block_keys, partner_block_turns).reshape((EVENTS, TOP))
    return dict(traces=traces, channel_valid=channel_valid, partner_block=partner_block)


def band_table(extent, lag_count):
    sample = jnp.arange(extent, dtype=jnp.int32)[:, None]
    shift = jnp.arange(lag_count, dtype=jnp.int32)[None, :]
    return ((sample >= shift) & (sample < shift + WIN)).astype(jnp.float32)

def reference(traces, channel_valid, partner_block):
    flat = partner_block.reshape(N_EVT, EV_DEV * TOP)
    owners = jnp.arange(N_EVT, dtype=jnp.int32)
    owner_hot = (flat[:, :, None] == owners[None, None, :]).astype(jnp.int32)
    before = jnp.cumsum(owner_hot, axis=1) - owner_hot
    ranking = lax.optimization_barrier(jnp.sum(before * owner_hot, axis=2))
    source = jnp.broadcast_to(owners[:, None], flat.shape)
    event_id = source * EV_DEV + jnp.arange(EV_DEV * TOP, dtype=jnp.int32)[None, :] // TOP
    lookup = jnp.full((N_EVT, SLOTS), -1, dtype=jnp.int32).at[flat, source * CAP + ranking].set(event_id)
    valid = channel_valid.astype(jnp.bfloat16)
    valid_wide = channel_valid.astype(jnp.float32)
    band = band_table(EXT, LAGS)

    def per_owner(owner):
        rows = lookup[owner]
        incoming = traces[jnp.maximum(rows, 0)] * (rows >= 0).astype(jnp.bfloat16)[:, None, None]
        block = lax.dynamic_slice_in_dim(traces, (owner * EV_DEV).astype(jnp.int32), EV_DEV, 0)
        template = block[:, :, MAXLAG:MAXLAG + WIN] * valid[None, :, None]
        flat_template = template.reshape(EV_DEV, CHANNELS * WIN)

        def one_lag(shift):
            window = lax.dynamic_slice_in_dim(incoming, shift.astype(jnp.int32), WIN, 2).reshape(SLOTS, CHANNELS * WIN)
            return jnp.dot(flat_template, window.T, preferred_element_type=jnp.float32)
        scores = lax.map(one_lag, jnp.arange(LAGS, dtype=jnp.int32))
        scores = jnp.transpose(scores, (1, 0, 2))
        event_energy = lax.optimization_barrier(jnp.sum(jnp.square(template.astype(jnp.float32)), axis=(1, 2)))
        squares_sum = lax.optimization_barrier(jnp.sum(jnp.square(incoming.astype(jnp.float32)) * valid_wide[None, :, None], axis=1))
        slot_energy = jnp.dot(squares_sum, band, precision=lax.Precision.HIGHEST)
        return scores / jnp.sqrt(event_energy[:, None, None] * slot_energy.T[None, :, :] + 1e-06)
    result = lax.map(per_owner, owners)
    return result.reshape(EVENTS, LAGS, SLOTS)
```

```python
import jax
import jax.numpy as jnp
from jax import lax
from jax.sharding import PartitionSpec as P

WIN = 200
MAXLAG = 40


def band_table(extent, lag_count):
    sample = jnp.arange(extent, dtype=jnp.int32)[:, None]
    shift = jnp.arange(lag_count, dtype=jnp.int32)[None, :]
    return ((sample >= shift) & (sample < shift + WIN)).astype(jnp.float32)


def body(traces, channel_valid, partner_block):
    events, channels, extent = traces.shape
    partners = partner_block.shape[1]
    devices_evt = lax.axis_size("evt")
    capacity = max(2, (events * partners + devices_evt - 1) // devices_evt)
    slot_count = devices_evt * capacity
    lag_count = extent - WIN + 1
    chunks = 4 if capacity % 4 == 0 else (2 if capacity % 2 == 0 else 1)
    per = capacity // chunks
    flat = partner_block.reshape(-1)
    owner_hot = (flat[:, None] == jnp.arange(devices_evt, dtype=jnp.int32)[None, :]).astype(
        jnp.int32
    )
    before = jnp.cumsum(owner_hot, axis=0) - owner_hot
    ranking = jnp.sum(before * owner_hot, axis=1)
    target = flat * capacity + ranking
    slot_hot = (target[:, None] == jnp.arange(slot_count, dtype=jnp.int32)[None, :]).astype(
        jnp.bfloat16
    )
    row_event = jnp.arange(events * partners, dtype=jnp.int32) // partners
    event_hot = (row_event[:, None] == jnp.arange(events, dtype=jnp.int32)[None, :]).astype(
        jnp.bfloat16
    )
    selection = jnp.dot(slot_hot.T, event_hot, preferred_element_type=jnp.float32).astype(
        jnp.bfloat16
    )
    outgoing = jnp.dot(
        selection, traces.reshape(events, channels * extent), preferred_element_type=jnp.float32
    ).astype(jnp.bfloat16)
    outgoing = outgoing.reshape(devices_evt, chunks, per, channels, extent)
    valid = channel_valid.astype(jnp.bfloat16)
    valid_wide = channel_valid.astype(jnp.float32)
    template = traces[:, :, MAXLAG : MAXLAG + WIN] * valid[None, :, None]
    event_energy = jnp.sum(jnp.square(template.astype(jnp.float32)), axis=(1, 2))
    band = band_table(extent, lag_count)
    width = devices_evt * per
    parts = []
    energies = []
    pending = None
    previous = None

    def reduce_pending(pending, previous):
        if previous is not None:
            previous, pending = lax.optimization_barrier((previous, pending))
            parts[-1] = (previous[:events], previous[events])
        total = lax.psum(pending, "sta")
        if not parts:
            energies.append(total[events + 1].reshape(-1)[:events])
        parts.append((total[:events], total[events]))
        return total

    for c in range(chunks):
        sending = outgoing[:, c].reshape(width, channels, extent)
        if pending is not None:
            pending, sending = lax.optimization_barrier((pending, sending))
        received = lax.all_to_all(sending, "evt", split_axis=0, concat_axis=0, tiled=True)
        if pending is not None:
            previous = reduce_pending(pending, previous)
        lag_scores = lax.conv_general_dilated(
            received,
            template,
            (1,),
            "VALID",
            dimension_numbers=("NCH", "OIH", "CHN"),
            preferred_element_type=jnp.float32,
        )
        squares_sum = jnp.sum(
            jnp.square(received.astype(jnp.float32)) * valid_wide[None, :, None], axis=1
        )
        slot_energy = lax.dot_general(
            band, squares_sum, (((0,), (1,)), ((), ())), precision=lax.Precision.HIGHEST
        )
        rows = [lag_scores, slot_energy[None]]
        if c == 0:
            pad = jnp.zeros((lag_count * width - events,), jnp.float32)
            rows.append(jnp.concatenate([event_energy, pad]).reshape(1, lag_count, width))
        pending = jnp.concatenate(rows, axis=0)
    previous = reduce_pending(pending, previous)
    energy_all = energies[0]
    outs = []
    for scores_all, slot_all in parts:
        outs.append(
            scores_all
            / jnp.sqrt(energy_all[:, None, None] * slot_all[None, :, :] + 1e-06)
        )
    coef = jnp.stack(outs, axis=0).reshape(chunks, events, lag_count, devices_evt, per)
    return jnp.transpose(coef, (1, 2, 3, 0, 4)).reshape(events, lag_count, slot_count)


def solution(mesh):
    return jax.shard_map(
        body,
        mesh=mesh,
        in_specs=(P("evt", "sta", None), P("sta"), P("evt", None)),
        out_specs=P("evt", None, None),
        check_vma=False,
    )
```

```python
import jax
import jax.numpy as jnp
from jax import lax
from jax.sharding import PartitionSpec as P

WIN = 200
MAXLAG = 40


def band_table(extent, lag_count):
    sample = jnp.arange(extent, dtype=jnp.int32)[:, None]
    shift = jnp.arange(lag_count, dtype=jnp.int32)[None, :]
    return ((sample >= shift) & (sample < shift + WIN)).astype(jnp.float32)


def normalize(lag_scores, slot_energy, event_energy):
    return lag_scores / jnp.sqrt(event_energy[:, None, None] * slot_energy[None, :, :] + 1e-06)


def exchange(value, axis, bit, size):
    return lax.ppermute(value, axis, [(i, i ^ bit) for i in range(size)])


def pick(pair, upper):
    return jnp.where(upper, pair[1], pair[0]), jnp.where(upper, pair[0], pair[1])


def place(mine, other, upper):
    return jnp.where(upper, jnp.stack([other, mine]), jnp.stack([mine, other]))


def halving_allreduce(data, axis, bits):
    size = lax.axis_size(axis)
    index = lax.axis_index(axis)
    uppers = [(index & bit) != 0 for bit in bits]
    acc = data
    for bit, upper in zip(bits, uppers):
        acc = acc.reshape((2, acc.shape[0] // 2) + acc.shape[1:])
        keep, send = pick(acc, upper)
        acc = keep + exchange(send, axis, bit, size)
    for bit, upper in zip(bits[::-1], uppers[::-1]):
        acc = place(acc, exchange(acc, axis, bit, size), upper)
        acc = acc.reshape((-1,) + acc.shape[2:])
    return acc


def sta_allreduce(data):
    size = lax.axis_size("sta")
    if size & (size - 1) or size == 1:
        return lax.psum(data, "sta")
    bits = [1 << k for k in range(size.bit_length() - 1)]
    half = data.shape[0] // 2
    first = halving_allreduce(data[:half], "sta", bits)
    second = halving_allreduce(data[half:], "sta", bits[::-1])
    return jnp.concatenate([first, second], axis=0)


def body(traces, channel_valid, partner_block):
    events, channels, extent = traces.shape
    partners = partner_block.shape[1]
    devices_evt = lax.axis_size("evt")
    sta_size = lax.axis_size("sta")
    capacity = max(2, (events * partners + devices_evt - 1) // devices_evt)
    slot_count = devices_evt * capacity
    lag_count = extent - WIN + 1
    flat = partner_block.reshape(-1)
    owner_hot = (flat[:, None] == jnp.arange(devices_evt, dtype=jnp.int32)[None, :]).astype(
        jnp.int32
    )
    before = jnp.cumsum(owner_hot, axis=0) - owner_hot
    ranking = jnp.sum(before * owner_hot, axis=1)
    target = flat * capacity + ranking
    slot_hot = (target[:, None] == jnp.arange(slot_count, dtype=jnp.int32)[None, :]).astype(
        jnp.bfloat16
    )
    row_event = jnp.arange(events * partners, dtype=jnp.int32) // partners
    event_hot = (row_event[:, None] == jnp.arange(events, dtype=jnp.int32)[None, :]).astype(
        jnp.bfloat16
    )
    selection = jnp.dot(slot_hot.T, event_hot, preferred_element_type=jnp.float32).astype(
        jnp.bfloat16
    )
    outgoing = jnp.dot(
        selection, traces.reshape(events, channels * extent), preferred_element_type=jnp.float32
    ).astype(jnp.bfloat16)
    received = lax.all_to_all(
        outgoing.reshape(slot_count, channels, extent),
        "evt",
        split_axis=0,
        concat_axis=0,
        tiled=True,
    )
    valid = channel_valid.astype(jnp.bfloat16)
    template = traces[:, :, MAXLAG : MAXLAG + WIN] * valid[None, :, None]
    lag_scores = lax.conv_general_dilated(
        received,
        template,
        (1,),
        "VALID",
        dimension_numbers=("NCH", "OIH", "CHN"),
        preferred_element_type=jnp.float32,
    )
    event_energy = jnp.sum(jnp.square(template.astype(jnp.float32)), axis=(1, 2))
    squares_sum = jnp.sum(
        jnp.square(received.astype(jnp.float32)) * channel_valid.astype(jnp.float32)[None, :, None],
        axis=1,
    )
    slot_energy = lax.dot_general(
        band_table(extent, lag_count),
        squares_sum,
        (((0,), (1,)), ((), ())),
        precision=lax.Precision.HIGHEST,
    )
    extra = 2 * sta_size
    pad = jnp.zeros((lag_count * slot_count - events,), jnp.float32)
    energy_row = jnp.concatenate([event_energy, pad]).reshape(1, lag_count, slot_count)
    filler = jnp.zeros((extra - 2, lag_count, slot_count), jnp.float32)
    packed = jnp.concatenate([lag_scores, slot_energy[None], energy_row, filler], axis=0)
    total = sta_allreduce(packed)
    event_all = total[events + 1].reshape(-1)[:events]
    return normalize(total[:events], total[events], event_all)


def solution(mesh):
    return jax.shard_map(
        body,
        mesh=mesh,
        in_specs=(P("evt", "sta", None), P("sta"), P("evt", None)),
        out_specs=P("evt", None, None),
        check_vma=False,
    )
```

```python
import jax
import jax.numpy as jnp
from jax import lax
from jax.sharding import PartitionSpec as P

WIN = 200
MAXLAG = 40


def band_table(extent, lag_count):
    sample = jnp.arange(extent, dtype=jnp.int32)[:, None]
    shift = jnp.arange(lag_count, dtype=jnp.int32)[None, :]
    return ((sample >= shift) & (sample < shift + WIN)).astype(jnp.float32)


def normalize(lag_scores, slot_energy, event_energy):
    return lag_scores / jnp.sqrt(event_energy[:, None, None] * slot_energy[None, :, :] + 1e-06)


def exchange(value, axis, bit, size):
    return lax.ppermute(value, axis, [(i, i ^ bit) for i in range(size)])


def pick(pair, upper):
    return jnp.where(upper, pair[1], pair[0]), jnp.where(upper, pair[0], pair[1])


def place(mine, other, upper):
    return jnp.where(upper, jnp.stack([other, mine]), jnp.stack([mine, other]))


def sta_allreduce(data):
    axis = "sta"
    size = lax.axis_size(axis)
    if size & (size - 1) or size == 1:
        return lax.psum(data, axis)
    index = lax.axis_index(axis)
    bits = [1 << k for k in range(size.bit_length() - 1)]
    orders = [bits, bits[::-1]]
    half = data.shape[0] // 2
    accs = [data[:half], data[half:]]
    for stage in range(len(bits)):
        sends, keeps = [], []
        for h in range(2):
            bit = orders[h][stage]
            acc = accs[h].reshape((2, accs[h].shape[0] // 2) + accs[h].shape[1:])
            keep, send = pick(acc, (index & bit) != 0)
            sends.append(send)
            keeps.append(keep)
        sends = lax.optimization_barrier(sends)
        got = [exchange(sends[h], axis, orders[h][stage], size) for h in range(2)]
        got = lax.optimization_barrier(got)
        accs = [keeps[h] + got[h] for h in range(2)]
    for stage in reversed(range(len(bits))):
        accs = lax.optimization_barrier(accs)
        got = [exchange(accs[h], axis, orders[h][stage], size) for h in range(2)]
        got = lax.optimization_barrier(got)
        accs = [
            place(accs[h], got[h], (index & orders[h][stage]) != 0).reshape(
                (-1,) + accs[h].shape[1:]
            )
            for h in range(2)
        ]
    return jnp.concatenate(accs, axis=0)


def body(traces, channel_valid, partner_block):
    events, channels, extent = traces.shape
    partners = partner_block.shape[1]
    devices_evt = lax.axis_size("evt")
    sta_size = lax.axis_size("sta")
    capacity = max(2, (events * partners + devices_evt - 1) // devices_evt)
    slot_count = devices_evt * capacity
    lag_count = extent - WIN + 1
    flat = partner_block.reshape(-1)
    owner_hot = (flat[:, None] == jnp.arange(devices_evt, dtype=jnp.int32)[None, :]).astype(
        jnp.int32
    )
    before = jnp.cumsum(owner_hot, axis=0) - owner_hot
    ranking = jnp.sum(before * owner_hot, axis=1)
    target = flat * capacity + ranking
    slot_hot = (target[:, None] == jnp.arange(slot_count, dtype=jnp.int32)[None, :]).astype(
        jnp.bfloat16
    )
    row_event = jnp.arange(events * partners, dtype=jnp.int32) // partners
    event_hot = (row_event[:, None] == jnp.arange(events, dtype=jnp.int32)[None, :]).astype(
        jnp.bfloat16
    )
    selection = jnp.dot(slot_hot.T, event_hot, preferred_element_type=jnp.float32).astype(
        jnp.bfloat16
    )
    outgoing = jnp.dot(
        selection, traces.reshape(events, channels * extent), preferred_element_type=jnp.float32
    ).astype(jnp.bfloat16)
    received = lax.all_to_all(
        outgoing.reshape(slot_count, channels, extent),
        "evt",
        split_axis=0,
        concat_axis=0,
        tiled=True,
    )
    valid = channel_valid.astype(jnp.bfloat16)
    template = traces[:, :, MAXLAG : MAXLAG + WIN] * valid[None, :, None]
    lag_scores = lax.conv_general_dilated(
        received,
        template,
        (1,),
        "VALID",
        dimension_numbers=("NCH", "OIH", "CHN"),
        preferred_element_type=jnp.float32,
    )
    event_energy = jnp.sum(jnp.square(template.astype(jnp.float32)), axis=(1, 2))
    squares_sum = jnp.sum(
        jnp.square(received.astype(jnp.float32)) * channel_valid.astype(jnp.float32)[None, :, None],
        axis=1,
    )
    slot_energy = lax.dot_general(
        band_table(extent, lag_count),
        squares_sum,
        (((0,), (1,)), ((), ())),
        precision=lax.Precision.HIGHEST,
    )
    extra = 2 * sta_size
    pad = jnp.zeros((lag_count * slot_count - events,), jnp.float32)
    energy_row = jnp.concatenate([event_energy, pad]).reshape(1, lag_count, slot_count)
    filler = jnp.zeros((extra - 2, lag_count, slot_count), jnp.float32)
    packed = jnp.concatenate([lag_scores, slot_energy[None], energy_row, filler], axis=0)
    total = sta_allreduce(packed)
    event_all = total[events + 1].reshape(-1)[:events]
    return normalize(total[:events], total[events], event_all)


def solution(mesh):
    return jax.shard_map(
        body,
        mesh=mesh,
        in_specs=(P("evt", "sta", None), P("sta"), P("evt", None)),
        out_specs=P("evt", None, None),
        check_vma=False,
    )
```

```python
import jax
import jax.numpy as jnp
from jax import lax
from jax.sharding import PartitionSpec as P

WIN = 200
MAXLAG = 40


def band_table(extent, lag_count):
    sample = jnp.arange(extent, dtype=jnp.int32)[:, None]
    shift = jnp.arange(lag_count, dtype=jnp.int32)[None, :]
    return ((sample >= shift) & (sample < shift + WIN)).astype(jnp.float32)


def normalize(lag_scores, slot_energy, event_energy):
    return lag_scores / jnp.sqrt(event_energy[:, None, None] * slot_energy[None, :, :] + 1e-06)


def exchange(value, axis, bit, size):
    return lax.ppermute(value, axis, [(i, i ^ bit) for i in range(size)])


def pick(pair, upper):
    return jnp.where(upper, pair[1], pair[0]), jnp.where(upper, pair[0], pair[1])


def place(mine, other, upper):
    return jnp.where(upper, jnp.stack([other, mine]), jnp.stack([mine, other]))


def sta_allreduce(data):
    axis = "sta"
    size = lax.axis_size(axis)
    if size & (size - 1) or size == 1:
        return lax.psum(data, axis)
    index = lax.axis_index(axis)
    bits = [1 << k for k in range(size.bit_length() - 1)]
    orders = [bits, bits[::-1]]
    half = data.shape[0] // 2
    accs = [data[:half], data[half:]]
    for stage in range(len(bits)):
        sends, keeps = [], []
        for h in range(2):
            bit = orders[h][stage]
            acc = accs[h].reshape((2, accs[h].shape[0] // 2) + accs[h].shape[1:])
            keep, send = pick(acc, (index & bit) != 0)
            sends.append(send)
            keeps.append(keep)
        sends = lax.optimization_barrier(sends)
        got = [exchange(sends[h], axis, orders[h][stage], size) for h in range(2)]
        got = lax.optimization_barrier(got)
        accs = [keeps[h] + got[h] for h in range(2)]
    for stage in reversed(range(len(bits))):
        accs = lax.optimization_barrier(accs)
        got = [exchange(accs[h], axis, orders[h][stage], size) for h in range(2)]
        got = lax.optimization_barrier(got)
        accs = [
            place(accs[h], got[h], (index & orders[h][stage]) != 0).reshape(
                (-1,) + accs[h].shape[1:]
            )
            for h in range(2)
        ]
    return jnp.concatenate(accs, axis=0)


def body(traces, channel_valid, partner_block):
    events, channels, extent = traces.shape
    partners = partner_block.shape[1]
    devices_evt = lax.axis_size("evt")
    sta_size = lax.axis_size("sta")
    capacity = max(2, (events * partners + devices_evt - 1) // devices_evt)
    slot_count = devices_evt * capacity
    lag_count = extent - WIN + 1
    flat = partner_block.reshape(-1)
    owner_hot = (flat[:, None] == jnp.arange(devices_evt, dtype=jnp.int32)[None, :]).astype(
        jnp.int32
    )
    before = jnp.cumsum(owner_hot, axis=0) - owner_hot
    ranking = jnp.sum(before * owner_hot, axis=1)
    target = flat * capacity + ranking
    slot_hot = (target[:, None] == jnp.arange(slot_count, dtype=jnp.int32)[None, :]).astype(
        jnp.bfloat16
    )
    row_event = jnp.arange(events * partners, dtype=jnp.int32) // partners
    event_hot = (row_event[:, None] == jnp.arange(events, dtype=jnp.int32)[None, :]).astype(
        jnp.bfloat16
    )
    selection = jnp.dot(slot_hot.T, event_hot, preferred_element_type=jnp.float32).astype(
        jnp.bfloat16
    )
    outgoing = jnp.dot(
        selection, traces.reshape(events, channels * extent), preferred_element_type=jnp.float32
    ).astype(jnp.bfloat16)
    chunks = 2 if capacity % 2 == 0 else 1
    per = capacity // chunks
    width = devices_evt * per
    outgoing = outgoing.reshape(devices_evt, chunks, per, channels, extent)
    valid = channel_valid.astype(jnp.bfloat16)
    valid_wide = channel_valid.astype(jnp.float32)
    template = traces[:, :, MAXLAG : MAXLAG + WIN] * valid[None, :, None]
    event_energy = jnp.sum(jnp.square(template.astype(jnp.float32)), axis=(1, 2))
    band = band_table(extent, lag_count)
    extra = 2 * sta_size
    totals = []
    packed = None
    for c in range(chunks):
        sending = outgoing[:, c].reshape(width, channels, extent)
        if packed is not None:
            packed, sending = lax.optimization_barrier((packed, sending))
            totals.append(sta_allreduce(packed))
        received = lax.all_to_all(
            sending,
            "evt",
            split_axis=0,
            concat_axis=0,
            tiled=True,
        )
        lag_scores = lax.conv_general_dilated(
            received,
            template,
            (1,),
            "VALID",
            dimension_numbers=("NCH", "OIH", "CHN"),
            preferred_element_type=jnp.float32,
        )
        squares_sum = jnp.sum(
            jnp.square(received.astype(jnp.float32)) * valid_wide[None, :, None], axis=1
        )
        slot_energy = lax.dot_general(
            band, squares_sum, (((0,), (1,)), ((), ())), precision=lax.Precision.HIGHEST
        )
        pad = jnp.zeros((lag_count * width - events,), jnp.float32)
        energy_row = jnp.concatenate([event_energy, pad]).reshape(1, lag_count, width)
        filler = jnp.zeros((extra - 2, lag_count, width), jnp.float32)
        packed = jnp.concatenate([lag_scores, slot_energy[None], energy_row, filler], axis=0)
    totals.append(sta_allreduce(packed))
    event_all = totals[0][events + 1].reshape(-1)[:events]
    coef = jnp.stack([normalize(t[:events], t[events], event_all) for t in totals], axis=0)
    coef = coef.reshape(chunks, events, lag_count, devices_evt, per)
    return jnp.transpose(coef, (1, 2, 3, 0, 4)).reshape(events, lag_count, slot_count)


def solution(mesh):
    return jax.shard_map(
        body,
        mesh=mesh,
        in_specs=(P("evt", "sta", None), P("sta"), P("evt", None)),
        out_specs=P("evt", None, None),
        check_vma=False,
    )
```

```python
import jax
import jax.numpy as jnp
from jax import lax
from jax.sharding import PartitionSpec as P

WIN = 200
MAXLAG = 40


def band_table(extent, lag_count):
    sample = jnp.arange(extent, dtype=jnp.int32)[:, None]
    shift = jnp.arange(lag_count, dtype=jnp.int32)[None, :]
    return ((sample >= shift) & (sample < shift + WIN)).astype(jnp.float32)


def normalize(lag_scores, slot_energy, event_energy):
    return lag_scores / jnp.sqrt(event_energy[:, None, None] * slot_energy[None, :, :] + 1e-06)


def exchange(value, axis, bit, size):
    return lax.ppermute(value, axis, [(i, i ^ bit) for i in range(size)])


def pick(pair, upper):
    return jnp.where(upper, pair[1], pair[0]), jnp.where(upper, pair[0], pair[1])


def place(mine, other, upper):
    return jnp.where(upper, jnp.stack([other, mine]), jnp.stack([mine, other]))


def sta_allreduce(data):
    axis = "sta"
    size = lax.axis_size(axis)
    if size & (size - 1) or size == 1:
        return lax.psum(data, axis)
    index = lax.axis_index(axis)
    bits = [1 << k for k in range(size.bit_length() - 1)]
    orders = [bits, bits[::-1]]
    half = data.shape[0] // 2
    accs = [data[:half], data[half:]]
    for stage in range(len(bits)):
        sends, keeps = [], []
        for h in range(2):
            bit = orders[h][stage]
            acc = accs[h].reshape((2, accs[h].shape[0] // 2) + accs[h].shape[1:])
            keep, send = pick(acc, (index & bit) != 0)
            sends.append(send)
            keeps.append(keep)
        sends = lax.optimization_barrier(sends)
        got = [exchange(sends[h], axis, orders[h][stage], size) for h in range(2)]
        got = lax.optimization_barrier(got)
        accs = [keeps[h] + got[h] for h in range(2)]
    for stage in reversed(range(len(bits))):
        accs = lax.optimization_barrier(accs)
        got = [exchange(accs[h], axis, orders[h][stage], size) for h in range(2)]
        got = lax.optimization_barrier(got)
        accs = [
            place(accs[h], got[h], (index & orders[h][stage]) != 0).reshape(
                (-1,) + accs[h].shape[1:]
            )
            for h in range(2)
        ]
    return jnp.concatenate(accs, axis=0)


def body(traces, channel_valid, partner_block):
    events, channels, extent = traces.shape
    partners = partner_block.shape[1]
    devices_evt = lax.axis_size("evt")
    sta_size = lax.axis_size("sta")
    capacity = max(2, (events * partners + devices_evt - 1) // devices_evt)
    slot_count = devices_evt * capacity
    lag_count = extent - WIN + 1
    flat = partner_block.reshape(-1)
    owner_hot = (flat[:, None] == jnp.arange(devices_evt, dtype=jnp.int32)[None, :]).astype(
        jnp.int32
    )
    before = jnp.cumsum(owner_hot, axis=0) - owner_hot
    ranking = jnp.sum(before * owner_hot, axis=1)
    target = flat * capacity + ranking
    slot_hot = (target[:, None] == jnp.arange(slot_count, dtype=jnp.int32)[None, :]).astype(
        jnp.bfloat16
    )
    row_event = jnp.arange(events * partners, dtype=jnp.int32) // partners
    event_hot = (row_event[:, None] == jnp.arange(events, dtype=jnp.int32)[None, :]).astype(
        jnp.bfloat16
    )
    selection = jnp.dot(slot_hot.T, event_hot, preferred_element_type=jnp.float32).astype(
        jnp.bfloat16
    )
    outgoing = jnp.dot(
        selection, traces.reshape(events, channels * extent), preferred_element_type=jnp.float32
    ).astype(jnp.bfloat16)
    chunks = 2 if capacity % 2 == 0 else 1
    per = capacity // chunks
    width = devices_evt * per
    outgoing = outgoing.reshape(devices_evt, chunks, per, channels, extent)
    valid = channel_valid.astype(jnp.bfloat16)
    valid_wide = channel_valid.astype(jnp.float32)
    template = traces[:, :, MAXLAG : MAXLAG + WIN] * valid[None, :, None]
    event_energy = jnp.sum(jnp.square(template.astype(jnp.float32)), axis=(1, 2))
    band = band_table(extent, lag_count)
    extra = 2 * sta_size
    totals = []
    packed = None
    for c in range(chunks):
        sending = outgoing[:, c].reshape(width, channels, extent)
        if packed is not None:
            packed, sending = lax.optimization_barrier((packed, sending))
            totals.append(sta_allreduce(packed))
        received = lax.all_to_all(
            sending,
            "evt",
            split_axis=0,
            concat_axis=0,
            tiled=True,
        )
        lag_scores = lax.conv_general_dilated(
            received,
            template,
            (1,),
            "VALID",
            dimension_numbers=("NCH", "OIH", "CHN"),
            preferred_element_type=jnp.float32,
        )
        squares_sum = jnp.sum(
            jnp.square(received.astype(jnp.float32)) * valid_wide[None, :, None], axis=1
        )
        slot_energy = lax.dot_general(
            band, squares_sum, (((0,), (1,)), ((), ())), precision=lax.Precision.HIGHEST
        )
        pad = jnp.zeros((lag_count * width - events,), jnp.float32)
        energy_row = jnp.concatenate([event_energy, pad]).reshape(1, lag_count, width)
        filler = jnp.zeros((extra - 2, lag_count, width), jnp.float32)
        packed = jnp.concatenate([lag_scores, slot_energy[None], energy_row, filler], axis=0)
        packed = packed.reshape(packed.shape[0], lag_count * width)
    totals.append(sta_allreduce(packed))
    totals = [t.reshape(t.shape[0], lag_count, width) for t in totals]
    event_all = totals[0][events + 1].reshape(-1)[:events]
    coef = jnp.stack([normalize(t[:events], t[events], event_all) for t in totals], axis=0)
    coef = coef.reshape(chunks, events, lag_count, devices_evt, per)
    return jnp.transpose(coef, (1, 2, 3, 0, 4)).reshape(events, lag_count, slot_count)


def solution(mesh):
    return jax.shard_map(
        body,
        mesh=mesh,
        in_specs=(P("evt", "sta", None), P("sta"), P("evt", None)),
        out_specs=P("evt", None, None),
        check_vma=False,
    )
```

```python
import jax
import jax.numpy as jnp
from jax import lax
from jax.sharding import PartitionSpec as P

WIN = 200
MAXLAG = 40


def band_table(extent, lag_count):
    sample = jnp.arange(extent, dtype=jnp.int32)[:, None]
    shift = jnp.arange(lag_count, dtype=jnp.int32)[None, :]
    return ((sample >= shift) & (sample < shift + WIN)).astype(jnp.float32)


def normalize(lag_scores, slot_energy, event_energy):
    return lag_scores / jnp.sqrt(event_energy[:, None, None] * slot_energy[None, :, :] + 1e-06)


def exchange(value, axis, bit, size):
    return lax.ppermute(value, axis, [(i, i ^ bit) for i in range(size)])


def pick(pair, upper):
    return jnp.where(upper, pair[1], pair[0]), jnp.where(upper, pair[0], pair[1])


def place(mine, other, upper):
    return jnp.where(upper, jnp.stack([other, mine]), jnp.stack([mine, other]))


def halving_allreduce(data, axis, bits):
    size = lax.axis_size(axis)
    index = lax.axis_index(axis)
    uppers = [(index & bit) != 0 for bit in bits]
    acc = data
    for bit, upper in zip(bits, uppers):
        acc = acc.reshape((2, acc.shape[0] // 2) + acc.shape[1:])
        keep, send = pick(acc, upper)
        acc = keep + exchange(send, axis, bit, size)
    for bit, upper in zip(bits[::-1], uppers[::-1]):
        acc = place(acc, exchange(acc, axis, bit, size), upper)
        acc = acc.reshape((-1,) + acc.shape[2:])
    return acc


def sta_allreduce(data, order):
    size = lax.axis_size("sta")
    if size & (size - 1) or size == 1:
        return lax.psum(data, "sta")
    bits = [1 << k for k in range(size.bit_length() - 1)]
    return halving_allreduce(data, "sta", bits[::-1] if order else bits)


def body(traces, channel_valid, partner_block):
    events, channels, extent = traces.shape
    partners = partner_block.shape[1]
    devices_evt = lax.axis_size("evt")
    sta_size = lax.axis_size("sta")
    capacity = max(2, (events * partners + devices_evt - 1) // devices_evt)
    slot_count = devices_evt * capacity
    lag_count = extent - WIN + 1
    flat = partner_block.reshape(-1)
    owner_hot = (flat[:, None] == jnp.arange(devices_evt, dtype=jnp.int32)[None, :]).astype(
        jnp.int32
    )
    before = jnp.cumsum(owner_hot, axis=0) - owner_hot
    ranking = jnp.sum(before * owner_hot, axis=1)
    target = flat * capacity + ranking
    slot_hot = (target[:, None] == jnp.arange(slot_count, dtype=jnp.int32)[None, :]).astype(
        jnp.bfloat16
    )
    row_event = jnp.arange(events * partners, dtype=jnp.int32) // partners
    event_hot = (row_event[:, None] == jnp.arange(events, dtype=jnp.int32)[None, :]).astype(
        jnp.bfloat16
    )
    selection = jnp.dot(slot_hot.T, event_hot, preferred_element_type=jnp.float32).astype(
        jnp.bfloat16
    )
    outgoing = jnp.dot(
        selection, traces.reshape(events, channels * extent), preferred_element_type=jnp.float32
    ).astype(jnp.bfloat16)
    received = lax.all_to_all(
        outgoing.reshape(slot_count, channels, extent),
        "evt",
        split_axis=0,
        concat_axis=0,
        tiled=True,
    )
    valid = channel_valid.astype(jnp.bfloat16)
    template = traces[:, :, MAXLAG : MAXLAG + WIN] * valid[None, :, None]
    event_energy = jnp.sum(jnp.square(template.astype(jnp.float32)), axis=(1, 2))
    squares_sum = jnp.sum(
        jnp.square(received.astype(jnp.float32)) * channel_valid.astype(jnp.float32)[None, :, None],
        axis=1,
    )
    slot_energy = lax.dot_general(
        band_table(extent, lag_count),
        squares_sum,
        (((0,), (1,)), ((), ())),
        precision=lax.Precision.HIGHEST,
    )
    pad = jnp.zeros((lag_count * slot_count - events,), jnp.float32)
    energy_row = jnp.concatenate([event_energy, pad]).reshape(1, lag_count, slot_count)
    split = events // 2
    totals = []
    for h, (low, high) in enumerate([(0, split), (split, events)]):
        lag_scores = lax.conv_general_dilated(
            received,
            template[low:high],
            (1,),
            "VALID",
            dimension_numbers=("NCH", "OIH", "CHN"),
            preferred_element_type=jnp.float32,
        )
        rows = [lag_scores]
        if h == 0:
            rows += [slot_energy[None], energy_row]
        count = sum(r.shape[0] for r in rows)
        spare = -count % sta_size
        if spare:
            rows.append(jnp.zeros((spare, lag_count, slot_count), jnp.float32))
        totals.append(sta_allreduce(jnp.concatenate(rows, axis=0), h))
    first, second = totals
    scores_all = jnp.concatenate([first[:split], second[: events - split]], axis=0)
    event_all = first[split + 1].reshape(-1)[:events]
    return normalize(scores_all, first[split], event_all)


def solution(mesh):
    return jax.shard_map(
        body,
        mesh=mesh,
        in_specs=(P("evt", "sta", None), P("sta"), P("evt", None)),
        out_specs=P("evt", None, None),
        check_vma=False,
    )
```

```python
import jax
import jax.numpy as jnp
from jax import lax
from jax.sharding import PartitionSpec as P

WIN = 200
MAXLAG = 40
FOLD = 4


def band_table(extent, lag_count):
    sample = jnp.arange(extent, dtype=jnp.int32)[:, None]
    shift = jnp.arange(lag_count, dtype=jnp.int32)[None, :]
    return ((sample >= shift) & (sample < shift + WIN)).astype(jnp.float32)


def normalize(lag_scores, slot_energy, event_energy):
    return lag_scores / jnp.sqrt(event_energy[:, None, None] * slot_energy[None, :, :] + 1e-06)


def exchange(value, axis, bit, size):
    return lax.ppermute(value, axis, [(i, i ^ bit) for i in range(size)])


def pick(pair, upper):
    return jnp.where(upper, pair[1], pair[0]), jnp.where(upper, pair[0], pair[1])


def place(mine, other, upper):
    return jnp.where(upper, jnp.stack([other, mine]), jnp.stack([mine, other]))


def sta_allreduce(data):
    axis = "sta"
    size = lax.axis_size(axis)
    if size & (size - 1) or size == 1:
        return lax.psum(data, axis)
    index = lax.axis_index(axis)
    bits = [1 << k for k in range(size.bit_length() - 1)]
    orders = [bits, bits[::-1]]
    half = data.shape[0] // 2
    accs = [data[:half], data[half:]]
    for stage in range(len(bits)):
        sends, keeps = [], []
        for h in range(2):
            bit = orders[h][stage]
            acc = accs[h].reshape((2, accs[h].shape[0] // 2) + accs[h].shape[1:])
            keep, send = pick(acc, (index & bit) != 0)
            sends.append(send)
            keeps.append(keep)
        sends = lax.optimization_barrier(sends)
        got = [exchange(sends[h], axis, orders[h][stage], size) for h in range(2)]
        got = lax.optimization_barrier(got)
        accs = [keeps[h] + got[h] for h in range(2)]
    for stage in reversed(range(len(bits))):
        accs = lax.optimization_barrier(accs)
        got = [exchange(accs[h], axis, orders[h][stage], size) for h in range(2)]
        got = lax.optimization_barrier(got)
        accs = [
            place(accs[h], got[h], (index & orders[h][stage]) != 0).reshape(
                (-1,) + accs[h].shape[1:]
            )
            for h in range(2)
        ]
    return jnp.concatenate(accs, axis=0)


def body(traces, channel_valid, partner_block):
    events, channels, extent = traces.shape
    partners = partner_block.shape[1]
    devices_evt = lax.axis_size("evt")
    sta_size = lax.axis_size("sta")
    capacity = max(2, (events * partners + devices_evt - 1) // devices_evt)
    slot_count = devices_evt * capacity
    lag_count = extent - WIN + 1
    flat = partner_block.reshape(-1)
    owner_hot = (flat[:, None] == jnp.arange(devices_evt, dtype=jnp.int32)[None, :]).astype(
        jnp.int32
    )
    before = jnp.cumsum(owner_hot, axis=0) - owner_hot
    ranking = jnp.sum(before * owner_hot, axis=1)
    target = flat * capacity + ranking
    slot_hot = (target[:, None] == jnp.arange(slot_count, dtype=jnp.int32)[None, :]).astype(
        jnp.bfloat16
    )
    row_event = jnp.arange(events * partners, dtype=jnp.int32) // partners
    event_hot = (row_event[:, None] == jnp.arange(events, dtype=jnp.int32)[None, :]).astype(
        jnp.bfloat16
    )
    selection = jnp.dot(slot_hot.T, event_hot, preferred_element_type=jnp.float32).astype(
        jnp.bfloat16
    )
    outgoing = jnp.dot(
        selection, traces.reshape(events, channels * extent), preferred_element_type=jnp.float32
    ).astype(jnp.bfloat16)
    received = lax.all_to_all(
        outgoing.reshape(slot_count, channels, extent),
        "evt",
        split_axis=0,
        concat_axis=0,
        tiled=True,
    )
    valid = channel_valid.astype(jnp.bfloat16)
    template = traces[:, :, MAXLAG : MAXLAG + WIN] * valid[None, :, None]
    fold = FOLD
    positions = -(-lag_count // fold)
    span = WIN + fold - 1
    reach = (positions - 1) * fold + span
    shifted = [
        jnp.pad(template, ((0, 0), (0, 0), (d, fold - 1 - d))) for d in range(fold)
    ]
    expanded = jnp.stack(shifted, axis=1).reshape(events * fold, channels, span)
    widened = jnp.pad(received, ((0, 0), (0, 0), (0, max(0, reach - extent))))
    lag_scores = lax.conv_general_dilated(
        widened,
        expanded,
        (fold,),
        "VALID",
        dimension_numbers=("NCH", "OIH", "CHN"),
        preferred_element_type=jnp.float32,
    ).reshape(events, fold, positions, slot_count)
    event_energy = jnp.sum(jnp.square(template.astype(jnp.float32)), axis=(1, 2))
    squares_sum = jnp.sum(
        jnp.square(received.astype(jnp.float32)) * channel_valid.astype(jnp.float32)[None, :, None],
        axis=1,
    )
    slot_energy = lax.dot_general(
        band_table(extent, lag_count),
        squares_sum,
        (((0,), (1,)), ((), ())),
        precision=lax.Precision.HIGHEST,
    )
    row = (fold, positions, slot_count)
    cells = fold * positions * slot_count
    slot_row = jnp.pad(slot_energy.reshape(-1), (0, cells - slot_energy.size)).reshape(row)
    energy_row = jnp.pad(event_energy, (0, cells - events)).reshape(row)
    extra = 2 * sta_size
    filler = jnp.zeros((extra - 2,) + row, jnp.float32)
    packed = jnp.concatenate([lag_scores, slot_row[None], energy_row[None], filler], axis=0)
    total = sta_allreduce(packed)
    event_all = total[events + 1].reshape(-1)[:events]
    slot_all = total[events].reshape(-1)[: lag_count * slot_count].reshape(lag_count, slot_count)
    scores_all = jnp.transpose(total[:events], (0, 2, 1, 3)).reshape(
        events, positions * fold, slot_count
    )[:, :lag_count]
    return normalize(scores_all, slot_all, event_all)


def solution(mesh):
    return jax.shard_map(
        body,
        mesh=mesh,
        in_specs=(P("evt", "sta", None), P("sta"), P("evt", None)),
        out_specs=P("evt", None, None),
        check_vma=False,
    )
```

```python
import jax
import jax.numpy as jnp
from jax import lax
from jax.experimental.layout import Layout, with_layout_constraint
from jax.sharding import PartitionSpec as P

WIN = 200
MAXLAG = 40
FOLD = 4


def band_table(extent, lag_count):
    sample = jnp.arange(extent, dtype=jnp.int32)[:, None]
    shift = jnp.arange(lag_count, dtype=jnp.int32)[None, :]
    return ((sample >= shift) & (sample < shift + WIN)).astype(jnp.float32)


def normalize(lag_scores, slot_energy, event_energy):
    return lag_scores / jnp.sqrt(event_energy[:, None, None] * slot_energy[None, :, :] + 1e-06)


def exchange(value, axis, bit, size):
    return lax.ppermute(value, axis, [(i, i ^ bit) for i in range(size)])


def pick(pair, upper):
    return jnp.where(upper, pair[1], pair[0]), jnp.where(upper, pair[0], pair[1])


def place(mine, other, upper):
    return jnp.where(upper, jnp.stack([other, mine]), jnp.stack([mine, other]))


def sta_allreduce(data):
    axis = "sta"
    size = lax.axis_size(axis)
    if size & (size - 1) or size == 1:
        return lax.psum(data, axis)
    index = lax.axis_index(axis)
    bits = [1 << k for k in range(size.bit_length() - 1)]
    orders = [bits, bits[::-1]]
    half = data.shape[0] // 2
    accs = [data[:half], data[half:]]
    for stage in range(len(bits)):
        sends, keeps = [], []
        for h in range(2):
            bit = orders[h][stage]
            acc = accs[h].reshape((2, accs[h].shape[0] // 2) + accs[h].shape[1:])
            keep, send = pick(acc, (index & bit) != 0)
            sends.append(send)
            keeps.append(keep)
        sends = lax.optimization_barrier(sends)
        got = [exchange(sends[h], axis, orders[h][stage], size) for h in range(2)]
        got = lax.optimization_barrier(got)
        accs = [keeps[h] + got[h] for h in range(2)]
    for stage in reversed(range(len(bits))):
        accs = lax.optimization_barrier(accs)
        got = [exchange(accs[h], axis, orders[h][stage], size) for h in range(2)]
        got = lax.optimization_barrier(got)
        accs = [
            place(accs[h], got[h], (index & orders[h][stage]) != 0).reshape(
                (-1,) + accs[h].shape[1:]
            )
            for h in range(2)
        ]
    return jnp.concatenate(accs, axis=0)


def body(traces, channel_valid, partner_block):
    events, channels, extent = traces.shape
    partners = partner_block.shape[1]
    devices_evt = lax.axis_size("evt")
    sta_size = lax.axis_size("sta")
    capacity = max(2, (events * partners + devices_evt - 1) // devices_evt)
    slot_count = devices_evt * capacity
    lag_count = extent - WIN + 1
    flat = partner_block.reshape(-1)
    owner_hot = (flat[:, None] == jnp.arange(devices_evt, dtype=jnp.int32)[None, :]).astype(
        jnp.int32
    )
    before = jnp.cumsum(owner_hot, axis=0) - owner_hot
    ranking = jnp.sum(before * owner_hot, axis=1)
    target = flat * capacity + ranking
    slot_hot = (target[:, None] == jnp.arange(slot_count, dtype=jnp.int32)[None, :]).astype(
        jnp.bfloat16
    )
    row_event = jnp.arange(events * partners, dtype=jnp.int32) // partners
    event_hot = (row_event[:, None] == jnp.arange(events, dtype=jnp.int32)[None, :]).astype(
        jnp.bfloat16
    )
    selection = jnp.dot(slot_hot.T, event_hot, preferred_element_type=jnp.float32).astype(
        jnp.bfloat16
    )
    outgoing = jnp.dot(
        selection, traces.reshape(events, channels * extent), preferred_element_type=jnp.float32
    ).astype(jnp.bfloat16)
    received = lax.all_to_all(
        outgoing.reshape(slot_count, channels, extent),
        "evt",
        split_axis=0,
        concat_axis=0,
        tiled=True,
    )
    valid = channel_valid.astype(jnp.bfloat16)
    template = traces[:, :, MAXLAG : MAXLAG + WIN] * valid[None, :, None]
    fold = FOLD
    positions = -(-lag_count // fold)
    span = WIN + fold - 1
    reach = (positions - 1) * fold + span
    shifted = [
        jnp.pad(template, ((0, 0), (0, 0), (d, fold - 1 - d))) for d in range(fold)
    ]
    expanded = jnp.stack(shifted, axis=1).reshape(events * fold, channels, span)
    widened = jnp.pad(received, ((0, 0), (0, 0), (0, max(0, reach - extent))))
    lag_scores = lax.conv_general_dilated(
        widened,
        expanded,
        (fold,),
        "VALID",
        dimension_numbers=("NCH", "OIH", "CHN"),
        preferred_element_type=jnp.float32,
    )
    lag_scores = with_layout_constraint(lag_scores, Layout((0, 1, 2)))
    event_energy = jnp.sum(jnp.square(template.astype(jnp.float32)), axis=(1, 2))
    squares_sum = jnp.sum(
        jnp.square(received.astype(jnp.float32)) * channel_valid.astype(jnp.float32)[None, :, None],
        axis=1,
    )
    slot_energy = lax.dot_general(
        band_table(extent, lag_count),
        squares_sum,
        (((0,), (1,)), ((), ())),
        precision=lax.Precision.HIGHEST,
    )
    cells = positions * slot_count
    slot_rows = -(-slot_energy.size // cells)
    energy_rows = -(-events // cells)
    used = events * fold + slot_rows + energy_rows
    spare = -used % (4 * sta_size)
    flat_slot = jnp.pad(slot_energy.reshape(-1), (0, slot_rows * cells - slot_energy.size))
    flat_event = jnp.pad(event_energy, (0, energy_rows * cells - events))
    packed = jnp.concatenate(
        [
            lag_scores,
            flat_slot.reshape(slot_rows, positions, slot_count),
            flat_event.reshape(energy_rows, positions, slot_count),
            jnp.zeros((spare, positions, slot_count), jnp.float32),
        ],
        axis=0,
    )
    total = sta_allreduce(packed)
    base = events * fold
    slot_all = total[base : base + slot_rows].reshape(-1)[: lag_count * slot_count]
    event_all = total[base + slot_rows : base + slot_rows + energy_rows].reshape(-1)[:events]
    scores_all = total[:base].reshape(events, fold, positions, slot_count)
    scores_all = jnp.transpose(scores_all, (0, 2, 1, 3)).reshape(
        events, positions * fold, slot_count
    )[:, :lag_count]
    return normalize(scores_all, slot_all.reshape(lag_count, slot_count), event_all)


def solution(mesh):
    return jax.shard_map(
        body,
        mesh=mesh,
        in_specs=(P("evt", "sta", None), P("sta"), P("evt", None)),
        out_specs=P("evt", None, None),
        check_vma=False,
    )
```

```python
import jax
import jax.numpy as jnp
from jax import lax
from jax.experimental.layout import Layout, with_layout_constraint
from jax.sharding import PartitionSpec as P

WIN = 200
MAXLAG = 40
FOLD = 4


def band_table(extent, lag_count):
    sample = jnp.arange(extent, dtype=jnp.int32)[:, None]
    shift = jnp.arange(lag_count, dtype=jnp.int32)[None, :]
    return ((sample >= shift) & (sample < shift + WIN)).astype(jnp.float32)


def normalize(lag_scores, slot_energy, event_energy):
    return lag_scores / jnp.sqrt(event_energy[:, None, None] * slot_energy[None, :, :] + 1e-06)


def exchange(value, axis, bit, size):
    return lax.ppermute(value, axis, [(i, i ^ bit) for i in range(size)])


def pick(pair, upper):
    return jnp.where(upper, pair[1], pair[0]), jnp.where(upper, pair[0], pair[1])


def place(mine, other, upper):
    return jnp.where(upper, jnp.stack([other, mine]), jnp.stack([mine, other]))


def sta_allreduce(data):
    axis = "sta"
    size = lax.axis_size(axis)
    if size & (size - 1) or size == 1:
        return lax.psum(data, axis)
    index = lax.axis_index(axis)
    bits = [1 << k for k in range(size.bit_length() - 1)]
    orders = [bits, bits[::-1]]
    half = data.shape[0] // 2
    accs = [data[:half], data[half:]]
    for stage in range(len(bits)):
        sends, keeps = [], []
        for h in range(2):
            bit = orders[h][stage]
            acc = accs[h].reshape((2, accs[h].shape[0] // 2) + accs[h].shape[1:])
            keep, send = pick(acc, (index & bit) != 0)
            sends.append(send)
            keeps.append(keep)
        sends = lax.optimization_barrier(sends)
        got = [exchange(sends[h], axis, orders[h][stage], size) for h in range(2)]
        got = lax.optimization_barrier(got)
        accs = [keeps[h] + got[h] for h in range(2)]
    for stage in reversed(range(len(bits))):
        accs = lax.optimization_barrier(accs)
        got = [exchange(accs[h], axis, orders[h][stage], size) for h in range(2)]
        got = lax.optimization_barrier(got)
        accs = [
            place(accs[h], got[h], (index & orders[h][stage]) != 0).reshape(
                (-1,) + accs[h].shape[1:]
            )
            for h in range(2)
        ]
    return jnp.concatenate(accs, axis=0)


def body(traces, channel_valid, partner_block):
    events, channels, extent = traces.shape
    partners = partner_block.shape[1]
    devices_evt = lax.axis_size("evt")
    sta_size = lax.axis_size("sta")
    capacity = max(2, (events * partners + devices_evt - 1) // devices_evt)
    slot_count = devices_evt * capacity
    lag_count = extent - WIN + 1
    flat = partner_block.reshape(-1)
    owner_hot = (flat[:, None] == jnp.arange(devices_evt, dtype=jnp.int32)[None, :]).astype(
        jnp.int32
    )
    before = jnp.cumsum(owner_hot, axis=0) - owner_hot
    ranking = jnp.sum(before * owner_hot, axis=1)
    target = flat * capacity + ranking
    slot_hot = (target[:, None] == jnp.arange(slot_count, dtype=jnp.int32)[None, :]).astype(
        jnp.bfloat16
    )
    row_event = jnp.arange(events * partners, dtype=jnp.int32) // partners
    event_hot = (row_event[:, None] == jnp.arange(events, dtype=jnp.int32)[None, :]).astype(
        jnp.bfloat16
    )
    selection = jnp.dot(slot_hot.T, event_hot, preferred_element_type=jnp.float32).astype(
        jnp.bfloat16
    )
    outgoing = jnp.dot(
        selection, traces.reshape(events, channels * extent), preferred_element_type=jnp.float32
    ).astype(jnp.bfloat16)
    chunks = 2 if capacity % 2 == 0 else 1
    per = capacity // chunks
    width = devices_evt * per
    outgoing = outgoing.reshape(devices_evt, chunks, per, channels, extent)
    valid = channel_valid.astype(jnp.bfloat16)
    valid_wide = channel_valid.astype(jnp.float32)
    template = traces[:, :, MAXLAG : MAXLAG + WIN] * valid[None, :, None]
    event_energy = jnp.sum(jnp.square(template.astype(jnp.float32)), axis=(1, 2))
    fold = FOLD
    positions = -(-lag_count // fold)
    span = WIN + fold - 1
    reach = (positions - 1) * fold + span
    shifted = [
        jnp.pad(template, ((0, 0), (0, 0), (d, fold - 1 - d))) for d in range(fold)
    ]
    expanded = jnp.stack(shifted, axis=1).reshape(events * fold, channels, span)
    band = band_table(extent, lag_count)
    cells = positions * width
    slot_rows = -(-(lag_count * width) // cells)
    energy_rows = -(-events // cells)
    base = events * fold
    used = base + slot_rows + energy_rows
    spare = -used % (4 * sta_size)
    totals = []
    packed = None
    for c in range(chunks):
        sending = outgoing[:, c].reshape(width, channels, extent)
        if packed is not None:
            packed, sending = lax.optimization_barrier((packed, sending))
            totals.append(sta_allreduce(packed))
        received = lax.all_to_all(sending, "evt", split_axis=0, concat_axis=0, tiled=True)
        widened = jnp.pad(received, ((0, 0), (0, 0), (0, max(0, reach - extent))))
        lag_scores = lax.conv_general_dilated(
            widened,
            expanded,
            (fold,),
            "VALID",
            dimension_numbers=("NCH", "OIH", "CHN"),
            preferred_element_type=jnp.float32,
        )
        lag_scores = with_layout_constraint(lag_scores, Layout((0, 1, 2)))
        squares_sum = jnp.sum(
            jnp.square(received.astype(jnp.float32)) * valid_wide[None, :, None], axis=1
        )
        slot_energy = lax.dot_general(
            band, squares_sum, (((0,), (1,)), ((), ())), precision=lax.Precision.HIGHEST
        )
        flat_slot = jnp.pad(slot_energy.reshape(-1), (0, slot_rows * cells - slot_energy.size))
        flat_event = jnp.pad(event_energy, (0, energy_rows * cells - events))
        packed = jnp.concatenate(
            [
                lag_scores.reshape(base, cells),
                flat_slot.reshape(slot_rows, cells),
                flat_event.reshape(energy_rows, cells),
                jnp.zeros((spare, cells), jnp.float32),
            ],
            axis=0,
        )
    totals.append(sta_allreduce(packed))
    event_all = totals[0][base + slot_rows : base + slot_rows + energy_rows].reshape(-1)[:events]
    outs = []
    for total in totals:
        slot_all = total[base : base + slot_rows].reshape(-1)[: lag_count * width]
        scores_all = total[:base].reshape(events, fold, positions, width)
        scores_all = jnp.transpose(scores_all, (0, 2, 1, 3)).reshape(
            events, positions * fold, width
        )[:, :lag_count]
        outs.append(normalize(scores_all, slot_all.reshape(lag_count, width), event_all))
    coef = jnp.stack(outs, axis=0).reshape(chunks, events, lag_count, devices_evt, per)
    return jnp.transpose(coef, (1, 2, 3, 0, 4)).reshape(events, lag_count, slot_count)


def solution(mesh):
    return jax.shard_map(
        body,
        mesh=mesh,
        in_specs=(P("evt", "sta", None), P("sta"), P("evt", None)),
        out_specs=P("evt", None, None),
        check_vma=False,
    )
```

```python
import jax
import jax.numpy as jnp
from jax import lax
from jax.experimental.layout import Layout, with_layout_constraint
from jax.sharding import PartitionSpec as P

WIN = 200
MAXLAG = 40
FOLD = 4


def band_table(extent, lag_count):
    sample = jnp.arange(extent, dtype=jnp.int32)[:, None]
    shift = jnp.arange(lag_count, dtype=jnp.int32)[None, :]
    return ((sample >= shift) & (sample < shift + WIN)).astype(jnp.float32)


def normalize(lag_scores, slot_energy, event_energy):
    return lag_scores / jnp.sqrt(event_energy[:, None, None] * slot_energy[None, :, :] + 1e-06)


def exchange(value, axis, bit, size):
    return lax.ppermute(value, axis, [(i, i ^ bit) for i in range(size)])


def pick(pair, upper):
    return jnp.where(upper, pair[1], pair[0]), jnp.where(upper, pair[0], pair[1])


def place(mine, other, upper):
    return jnp.where(upper, jnp.stack([other, mine]), jnp.stack([mine, other]))


def sta_allreduce(data):
    axis = "sta"
    size = lax.axis_size(axis)
    if size & (size - 1) or size == 1:
        return lax.psum(data, axis)
    index = lax.axis_index(axis)
    bits = [1 << k for k in range(size.bit_length() - 1)]
    orders = [bits, bits[::-1]]
    half = data.shape[0] // 2
    accs = [data[:half], data[half:]]
    for stage in range(len(bits)):
        sends, keeps = [], []
        for h in range(2):
            bit = orders[h][stage]
            acc = accs[h].reshape((2, accs[h].shape[0] // 2) + accs[h].shape[1:])
            keep, send = pick(acc, (index & bit) != 0)
            sends.append(send)
            keeps.append(keep)
        sends = lax.optimization_barrier(sends)
        got = [exchange(sends[h], axis, orders[h][stage], size) for h in range(2)]
        got = lax.optimization_barrier(got)
        accs = [keeps[h] + got[h] for h in range(2)]
    for stage in reversed(range(len(bits))):
        accs = lax.optimization_barrier(accs)
        got = [exchange(accs[h], axis, orders[h][stage], size) for h in range(2)]
        got = lax.optimization_barrier(got)
        accs = [
            place(accs[h], got[h], (index & orders[h][stage]) != 0).reshape(
                (-1,) + accs[h].shape[1:]
            )
            for h in range(2)
        ]
    return jnp.concatenate(accs, axis=0)


def body(traces, channel_valid, partner_block):
    events, channels, extent = traces.shape
    partners = partner_block.shape[1]
    devices_evt = lax.axis_size("evt")
    sta_size = lax.axis_size("sta")
    capacity = max(2, (events * partners + devices_evt - 1) // devices_evt)
    slot_count = devices_evt * capacity
    lag_count = extent - WIN + 1
    flat = partner_block.reshape(-1)
    owner_hot = (flat[:, None] == jnp.arange(devices_evt, dtype=jnp.int32)[None, :]).astype(
        jnp.int32
    )
    before = jnp.cumsum(owner_hot, axis=0) - owner_hot
    ranking = jnp.sum(before * owner_hot, axis=1)
    target = flat * capacity + ranking
    slot_hot = (target[:, None] == jnp.arange(slot_count, dtype=jnp.int32)[None, :]).astype(
        jnp.bfloat16
    )
    row_event = jnp.arange(events * partners, dtype=jnp.int32) // partners
    event_hot = (row_event[:, None] == jnp.arange(events, dtype=jnp.int32)[None, :]).astype(
        jnp.bfloat16
    )
    selection = jnp.dot(slot_hot.T, event_hot, preferred_element_type=jnp.float32).astype(
        jnp.bfloat16
    )
    outgoing = lax.dot_general(
        selection, traces, (((1,), (0,)), ((), ())), preferred_element_type=jnp.float32
    ).astype(jnp.bfloat16)
    received = lax.all_to_all(
        outgoing,
        "evt",
        split_axis=0,
        concat_axis=0,
        tiled=True,
    )
    valid = channel_valid.astype(jnp.bfloat16)
    template = traces[:, :, MAXLAG : MAXLAG + WIN] * valid[None, :, None]
    fold = FOLD
    positions = -(-lag_count // fold)
    span = WIN + fold - 1
    reach = (positions - 1) * fold + span
    shifted = [
        jnp.pad(template, ((0, 0), (0, 0), (d, fold - 1 - d))) for d in range(fold)
    ]
    expanded = jnp.stack(shifted, axis=1).reshape(events * fold, channels, span)
    widened = jnp.pad(received, ((0, 0), (0, 0), (0, max(0, reach - extent))))
    lag_scores = lax.conv_general_dilated(
        widened,
        expanded,
        (fold,),
        "VALID",
        dimension_numbers=("NCH", "OIH", "CHN"),
        preferred_element_type=jnp.float32,
    )
    lag_scores = with_layout_constraint(lag_scores, Layout((0, 1, 2)))
    event_energy = jnp.sum(jnp.square(template.astype(jnp.float32)), axis=(1, 2))
    squares_sum = jnp.sum(
        jnp.square(received.astype(jnp.float32)) * channel_valid.astype(jnp.float32)[None, :, None],
        axis=1,
    )
    slot_energy = lax.dot_general(
        band_table(extent, lag_count),
        squares_sum,
        (((0,), (1,)), ((), ())),
        precision=lax.Precision.HIGHEST,
    )
    cells = positions * slot_count
    slot_rows = -(-slot_energy.size // cells)
    energy_rows = -(-events // cells)
    used = events * fold + slot_rows + energy_rows
    spare = -used % (2 * sta_size)
    flat_slot = jnp.pad(slot_energy.reshape(-1), (0, slot_rows * cells - slot_energy.size))
    flat_event = jnp.pad(event_energy, (0, energy_rows * cells - events))
    packed = jnp.concatenate(
        [
            lag_scores,
            flat_slot.reshape(slot_rows, positions, slot_count),
            flat_event.reshape(energy_rows, positions, slot_count),
            jnp.zeros((spare, positions, slot_count), jnp.float32),
        ],
        axis=0,
    )
    total = sta_allreduce(packed)
    base = events * fold
    slot_all = total[base : base + slot_rows].reshape(-1)[: lag_count * slot_count]
    event_all = total[base + slot_rows : base + slot_rows + energy_rows].reshape(-1)[:events]
    scores_all = total[:base].reshape(events, fold, positions, slot_count)
    scores_all = jnp.transpose(scores_all, (0, 2, 1, 3)).reshape(
        events, positions * fold, slot_count
    )[:, :lag_count]
    return normalize(scores_all, slot_all.reshape(lag_count, slot_count), event_all)


def solution(mesh):
    return jax.shard_map(
        body,
        mesh=mesh,
        in_specs=(P("evt", "sta", None), P("sta"), P("evt", None)),
        out_specs=P("evt", None, None),
        check_vma=False,
    )
```

```python
import jax
import jax.numpy as jnp
from jax import lax
from jax.experimental.layout import Layout, with_layout_constraint
from jax.sharding import PartitionSpec as P

WIN = 200
MAXLAG = 40
FOLD = 4


def band_table(extent, lag_count):
    sample = jnp.arange(extent, dtype=jnp.int32)[:, None]
    shift = jnp.arange(lag_count, dtype=jnp.int32)[None, :]
    return ((sample >= shift) & (sample < shift + WIN)).astype(jnp.float32)


def normalize(lag_scores, slot_energy, event_energy):
    return lag_scores / jnp.sqrt(event_energy[:, None, None] * slot_energy[None, :, :] + 1e-06)


def exchange(value, axis, bit, size):
    return lax.ppermute(value, axis, [(i, i ^ bit) for i in range(size)])


def pick(pair, upper):
    return jnp.where(upper, pair[1], pair[0]), jnp.where(upper, pair[0], pair[1])


def place(mine, other, upper):
    return jnp.where(upper, jnp.stack([other, mine]), jnp.stack([mine, other]))


def sta_allreduce(data):
    axis = "sta"
    size = lax.axis_size(axis)
    if size & (size - 1) or size == 1:
        return lax.psum(data, axis)
    index = lax.axis_index(axis)
    bits = [1 << k for k in range(size.bit_length() - 1)]
    orders = [bits, bits[::-1]]
    half = data.shape[0] // 2
    accs = [data[:half], data[half:]]
    for stage in range(len(bits)):
        sends, keeps = [], []
        for h in range(2):
            bit = orders[h][stage]
            acc = accs[h].reshape((2, accs[h].shape[0] // 2) + accs[h].shape[1:])
            keep, send = pick(acc, (index & bit) != 0)
            sends.append(send)
            keeps.append(keep)
        sends = lax.optimization_barrier(sends)
        got = [exchange(sends[h], axis, orders[h][stage], size) for h in range(2)]
        got = lax.optimization_barrier(got)
        accs = [keeps[h] + got[h] for h in range(2)]
    for stage in reversed(range(len(bits))):
        accs = lax.optimization_barrier(accs)
        got = [exchange(accs[h], axis, orders[h][stage], size) for h in range(2)]
        got = lax.optimization_barrier(got)
        accs = [
            place(accs[h], got[h], (index & orders[h][stage]) != 0).reshape(
                (-1,) + accs[h].shape[1:]
            )
            for h in range(2)
        ]
    return jnp.concatenate(accs, axis=0)


def body(traces, channel_valid, partner_block):
    events, channels, extent = traces.shape
    partners = partner_block.shape[1]
    devices_evt = lax.axis_size("evt")
    sta_size = lax.axis_size("sta")
    capacity = max(2, (events * partners + devices_evt - 1) // devices_evt)
    slot_count = devices_evt * capacity
    lag_count = extent - WIN + 1
    flat = partner_block.reshape(-1)
    owner_hot = (flat[:, None] == jnp.arange(devices_evt, dtype=jnp.int32)[None, :]).astype(
        jnp.int32
    )
    before = jnp.cumsum(owner_hot, axis=0) - owner_hot
    ranking = jnp.sum(before * owner_hot, axis=1)
    target = flat * capacity + ranking
    slot_hot = target[:, None] == jnp.arange(slot_count, dtype=jnp.int32)[None, :]
    row_event = jnp.arange(events * partners, dtype=jnp.int32) // partners
    filled = jnp.any(slot_hot, axis=0)
    source = jnp.sum(jnp.where(slot_hot, row_event[:, None], 0), axis=0)
    outgoing = jnp.take(traces, source, axis=0) * filled.astype(jnp.bfloat16)[:, None, None]
    received = lax.all_to_all(
        outgoing,
        "evt",
        split_axis=0,
        concat_axis=0,
        tiled=True,
    )
    received = with_layout_constraint(received, Layout((2, 1, 0)))
    valid = channel_valid.astype(jnp.bfloat16)
    template = traces[:, :, MAXLAG : MAXLAG + WIN] * valid[None, :, None]
    fold = FOLD
    positions = -(-lag_count // fold)
    span = WIN + fold - 1
    reach = (positions - 1) * fold + span
    shifted = [
        jnp.pad(template, ((0, 0), (0, 0), (d, fold - 1 - d))) for d in range(fold)
    ]
    expanded = jnp.stack(shifted, axis=1).reshape(events * fold, channels, span)
    widened = jnp.pad(received, ((0, 0), (0, 0), (0, max(0, reach - extent))))
    lag_scores = lax.conv_general_dilated(
        widened,
        expanded,
        (fold,),
        "VALID",
        dimension_numbers=("NCH", "OIH", "CHN"),
        preferred_element_type=jnp.float32,
    )
    lag_scores = with_layout_constraint(lag_scores, Layout((0, 1, 2)))
    event_energy = jnp.sum(jnp.square(template.astype(jnp.float32)), axis=(1, 2))
    squares_sum = jnp.sum(
        jnp.square(received.astype(jnp.float32)) * channel_valid.astype(jnp.float32)[None, :, None],
        axis=1,
    )
    slot_energy = lax.dot_general(
        band_table(extent, lag_count),
        squares_sum,
        (((0,), (1,)), ((), ())),
        precision=lax.Precision.HIGHEST,
    )
    cells = positions * slot_count
    slot_rows = -(-slot_energy.size // cells)
    energy_rows = -(-events // cells)
    used = events * fold + slot_rows + energy_rows
    spare = -used % (2 * sta_size)
    flat_slot = jnp.pad(slot_energy.reshape(-1), (0, slot_rows * cells - slot_energy.size))
    flat_event = jnp.pad(event_energy, (0, energy_rows * cells - events))
    packed = jnp.concatenate(
        [
            lag_scores,
            flat_slot.reshape(slot_rows, positions, slot_count),
            flat_event.reshape(energy_rows, positions, slot_count),
            jnp.zeros((spare, positions, slot_count), jnp.float32),
        ],
        axis=0,
    )
    total = sta_allreduce(packed)
    base = events * fold
    slot_all = total[base : base + slot_rows].reshape(-1)[: lag_count * slot_count]
    event_all = total[base + slot_rows : base + slot_rows + energy_rows].reshape(-1)[:events]
    scores_all = total[:base].reshape(events, fold, positions, slot_count)
    scores_all = jnp.transpose(scores_all, (0, 2, 1, 3)).reshape(
        events, positions * fold, slot_count
    )[:, :lag_count]
    return normalize(scores_all, slot_all.reshape(lag_count, slot_count), event_all)


def solution(mesh):
    return jax.shard_map(
        body,
        mesh=mesh,
        in_specs=(P("evt", "sta", None), P("sta"), P("evt", None)),
        out_specs=P("evt", None, None),
        check_vma=False,
    )
```

```python
import jax
import jax.numpy as jnp
from jax import lax
from jax.experimental.layout import Layout, with_layout_constraint
from jax.sharding import PartitionSpec as P

WIN = 200
MAXLAG = 40
FOLD = 4


def band_table(extent, lag_count):
    sample = jnp.arange(extent, dtype=jnp.int32)[:, None]
    shift = jnp.arange(lag_count, dtype=jnp.int32)[None, :]
    return ((sample >= shift) & (sample < shift + WIN)).astype(jnp.float32)


def normalize(lag_scores, slot_energy, event_energy):
    return lag_scores / jnp.sqrt(event_energy[:, None, None] * slot_energy[None, :, :] + 1e-06)


def exchange(value, axis, bit, size):
    return lax.ppermute(value, axis, [(i, i ^ bit) for i in range(size)])


def pick(pair, upper):
    return jnp.where(upper, pair[1], pair[0]), jnp.where(upper, pair[0], pair[1])


def place(mine, other, upper):
    return jnp.where(upper, jnp.stack([other, mine]), jnp.stack([mine, other]))


def sta_allreduce(data):
    axis = "sta"
    size = lax.axis_size(axis)
    if size & (size - 1) or size == 1:
        return lax.psum(data, axis)
    index = lax.axis_index(axis)
    bits = [1 << k for k in range(size.bit_length() - 1)]
    orders = [bits, bits[::-1]]
    half = data.shape[0] // 2
    accs = [data[:half], data[half:]]
    for stage in range(len(bits)):
        sends, keeps = [], []
        for h in range(2):
            bit = orders[h][stage]
            acc = accs[h].reshape((2, accs[h].shape[0] // 2) + accs[h].shape[1:])
            keep, send = pick(acc, (index & bit) != 0)
            sends.append(send)
            keeps.append(keep)
        sends = lax.optimization_barrier(sends)
        got = [exchange(sends[h], axis, orders[h][stage], size) for h in range(2)]
        got = lax.optimization_barrier(got)
        accs = [keeps[h] + got[h] for h in range(2)]
    for stage in reversed(range(len(bits))):
        accs = lax.optimization_barrier(accs)
        got = [exchange(accs[h], axis, orders[h][stage], size) for h in range(2)]
        got = lax.optimization_barrier(got)
        accs = [
            place(accs[h], got[h], (index & orders[h][stage]) != 0).reshape(
                (-1,) + accs[h].shape[1:]
            )
            for h in range(2)
        ]
    return jnp.concatenate(accs, axis=0)


def body(traces, channel_valid, partner_block):
    events, channels, extent = traces.shape
    partners = partner_block.shape[1]
    devices_evt = lax.axis_size("evt")
    sta_size = lax.axis_size("sta")
    capacity = max(2, (events * partners + devices_evt - 1) // devices_evt)
    slot_count = devices_evt * capacity
    lag_count = extent - WIN + 1
    flat = partner_block.reshape(-1)
    owner_hot = (flat[:, None] == jnp.arange(devices_evt, dtype=jnp.int32)[None, :]).astype(
        jnp.int32
    )
    before = jnp.cumsum(owner_hot, axis=0) - owner_hot
    ranking = jnp.sum(before * owner_hot, axis=1)
    target = flat * capacity + ranking
    slot_hot = target[:, None] == jnp.arange(slot_count, dtype=jnp.int32)[None, :]
    row_event = jnp.arange(events * partners, dtype=jnp.int32) // partners
    filled = jnp.any(slot_hot, axis=0)
    source = jnp.sum(jnp.where(slot_hot, row_event[:, None], 0), axis=0)
    outgoing = jnp.take(traces, source, axis=0) * filled.astype(jnp.bfloat16)[:, None, None]
    evt_index = lax.axis_index("evt")
    half = devices_evt // 2
    low = evt_index % half
    upper_half = evt_index // half
    blocks = outgoing.reshape(devices_evt, capacity, channels, extent)
    order = jnp.arange(half, dtype=jnp.int32) ^ low
    valid = channel_valid.astype(jnp.bfloat16)
    valid_wide = channel_valid.astype(jnp.float32)
    template = traces[:, :, MAXLAG : MAXLAG + WIN] * valid[None, :, None]
    event_energy = jnp.sum(jnp.square(template.astype(jnp.float32)), axis=(1, 2))
    fold = FOLD
    positions = -(-lag_count // fold)
    span = WIN + fold - 1
    reach = (positions - 1) * fold + span
    shifted = [
        jnp.pad(template, ((0, 0), (0, 0), (d, fold - 1 - d))) for d in range(fold)
    ]
    expanded = jnp.stack(shifted, axis=1).reshape(events * fold, channels, span)
    band = band_table(extent, lag_count)
    width = half * capacity
    cells = positions * width
    slot_rows = -(-(lag_count * width) // cells)
    energy_rows = -(-events // cells)
    base = events * fold
    used = base + slot_rows + energy_rows
    spare = -used % (2 * sta_size)
    pieces = [
        lax.dynamic_index_in_dim(blocks, evt_index ^ k, 0, keepdims=False)
        for k in range(devices_evt)
    ]
    totals = []
    packed = None
    for c in range(2):
        sends = pieces[c * half : (c + 1) * half]
        if packed is not None:
            packed, sends = lax.optimization_barrier((packed, sends))
            totals.append(sta_allreduce(packed))
        got = [
            lax.ppermute(piece, "evt", [(i, i ^ k) for i in range(devices_evt)]) if k else piece
            for k, piece in zip(range(c * half, (c + 1) * half), sends)
        ]
        arrived = jnp.stack(got)
        received = jnp.take(arrived, order, axis=0).reshape(width, channels, extent)
        received = with_layout_constraint(received, Layout((2, 1, 0)))
        widened = jnp.pad(received, ((0, 0), (0, 0), (0, max(0, reach - extent))))
        lag_scores = lax.conv_general_dilated(
            widened,
            expanded,
            (fold,),
            "VALID",
            dimension_numbers=("NCH", "OIH", "CHN"),
            preferred_element_type=jnp.float32,
        )
        lag_scores = with_layout_constraint(lag_scores, Layout((0, 1, 2)))
        squares_sum = jnp.sum(
            jnp.square(received.astype(jnp.float32)) * valid_wide[None, :, None], axis=1
        )
        slot_energy = lax.dot_general(
            band, squares_sum, (((0,), (1,)), ((), ())), precision=lax.Precision.HIGHEST
        )
        flat_slot = jnp.pad(slot_energy.reshape(-1), (0, slot_rows * cells - slot_energy.size))
        flat_event = jnp.pad(event_energy, (0, energy_rows * cells - events))
        packed = jnp.concatenate(
            [
                lag_scores.reshape(base, cells),
                flat_slot.reshape(slot_rows, cells),
                flat_event.reshape(energy_rows, cells),
                jnp.zeros((spare, cells), jnp.float32),
            ],
            axis=0,
        )
    totals.append(sta_allreduce(packed))
    event_all = totals[0][base + slot_rows : base + slot_rows + energy_rows].reshape(-1)[:events]
    outs = []
    for total in totals:
        slot_all = total[base : base + slot_rows].reshape(-1)[: lag_count * width]
        scores_all = total[:base].reshape(events, fold, positions, width)
        scores_all = jnp.transpose(scores_all, (0, 2, 1, 3)).reshape(
            events, positions * fold, width
        )[:, :lag_count]
        outs.append(normalize(scores_all, slot_all.reshape(lag_count, width), event_all))
    first, second = outs
    return jnp.where(
        upper_half == 0,
        jnp.concatenate([first, second], axis=2),
        jnp.concatenate([second, first], axis=2),
    )


def solution(mesh):
    return jax.shard_map(
        body,
        mesh=mesh,
        in_specs=(P("evt", "sta", None), P("sta"), P("evt", None)),
        out_specs=P("evt", None, None),
        check_vma=False,
    )
```

```python
import jax
import jax.numpy as jnp
from jax import lax
from jax.experimental.layout import Layout, with_layout_constraint
from jax.sharding import PartitionSpec as P

WIN = 200
MAXLAG = 40
FOLD = 4


def band_table(extent, lag_count):
    sample = jnp.arange(extent, dtype=jnp.int32)[:, None]
    shift = jnp.arange(lag_count, dtype=jnp.int32)[None, :]
    return ((sample >= shift) & (sample < shift + WIN)).astype(jnp.float32)


def normalize(lag_scores, slot_energy, event_energy):
    return lag_scores / jnp.sqrt(event_energy[:, None, None] * slot_energy[None, :, :] + 1e-06)


def exchange(value, axis, bit, size):
    return lax.ppermute(value, axis, [(i, i ^ bit) for i in range(size)])


def pick(pair, upper):
    return jnp.where(upper, pair[1], pair[0]), jnp.where(upper, pair[0], pair[1])


def place(mine, other, upper):
    return jnp.where(upper, jnp.stack([other, mine]), jnp.stack([mine, other]))


def sta_allreduce(data):
    axis = "sta"
    size = lax.axis_size(axis)
    if size & (size - 1) or size == 1:
        return lax.psum(data, axis)
    index = lax.axis_index(axis)
    bits = [1 << k for k in range(size.bit_length() - 1)]
    orders = [bits, bits[::-1]]
    half = data.shape[0] // 2
    accs = [data[:half], data[half:]]
    for stage in range(len(bits)):
        sends, keeps = [], []
        for h in range(2):
            bit = orders[h][stage]
            acc = accs[h].reshape((2, accs[h].shape[0] // 2) + accs[h].shape[1:])
            keep, send = pick(acc, (index & bit) != 0)
            sends.append(send)
            keeps.append(keep)
        sends = lax.optimization_barrier(sends)
        got = [exchange(sends[h], axis, orders[h][stage], size) for h in range(2)]
        got = lax.optimization_barrier(got)
        accs = [keeps[h] + got[h] for h in range(2)]
    for stage in reversed(range(len(bits))):
        accs = lax.optimization_barrier(accs)
        got = [exchange(accs[h], axis, orders[h][stage], size) for h in range(2)]
        got = lax.optimization_barrier(got)
        accs = [
            place(accs[h], got[h], (index & orders[h][stage]) != 0).reshape(
                (-1,) + accs[h].shape[1:]
            )
            for h in range(2)
        ]
    return jnp.concatenate(accs, axis=0)


def body(traces, channel_valid, partner_block):
    events, channels, extent = traces.shape
    partners = partner_block.shape[1]
    devices_evt = lax.axis_size("evt")
    sta_size = lax.axis_size("sta")
    capacity = max(2, (events * partners + devices_evt - 1) // devices_evt)
    slot_count = devices_evt * capacity
    lag_count = extent - WIN + 1
    flat = partner_block.reshape(-1)
    owner_hot = (flat[:, None] == jnp.arange(devices_evt, dtype=jnp.int32)[None, :]).astype(
        jnp.int32
    )
    before = jnp.cumsum(owner_hot, axis=0) - owner_hot
    ranking = jnp.sum(before * owner_hot, axis=1)
    target = flat * capacity + ranking
    slot_hot = target[:, None] == jnp.arange(slot_count, dtype=jnp.int32)[None, :]
    row_event = jnp.arange(events * partners, dtype=jnp.int32) // partners
    filled = jnp.any(slot_hot, axis=0)
    source = jnp.sum(jnp.where(slot_hot, row_event[:, None], 0), axis=0)
    outgoing = jnp.take(traces, source, axis=0) * filled.astype(jnp.bfloat16)[:, None, None]
    received = lax.all_to_all(
        outgoing,
        "evt",
        split_axis=0,
        concat_axis=0,
        tiled=True,
    )
    received = with_layout_constraint(received, Layout((2, 1, 0)))
    valid = channel_valid.astype(jnp.bfloat16)
    template = traces[:, :, MAXLAG : MAXLAG + WIN] * valid[None, :, None]
    fold = FOLD
    positions = -(-lag_count // fold)
    span = WIN + fold - 1
    reach = (positions - 1) * fold + span
    shifted = [
        jnp.pad(template, ((0, 0), (0, 0), (d, fold - 1 - d))) for d in range(fold)
    ]
    expanded = jnp.stack(shifted, axis=1).reshape(events * fold, channels, span)
    widened = jnp.pad(received, ((0, 0), (0, 0), (0, max(0, reach - extent))))
    lag_scores = lax.conv_general_dilated(
        widened,
        expanded,
        (fold,),
        "VALID",
        dimension_numbers=("NCH", "OIH", "CHN"),
        preferred_element_type=jnp.float32,
    )
    lag_scores = with_layout_constraint(lag_scores, Layout((1, 0, 2)))
    event_energy = jnp.sum(jnp.square(template.astype(jnp.float32)), axis=(1, 2))
    squares_sum = jnp.sum(
        jnp.square(received.astype(jnp.float32)) * channel_valid.astype(jnp.float32)[None, :, None],
        axis=1,
    )
    slot_energy = lax.dot_general(
        band_table(extent, lag_count),
        squares_sum,
        (((0,), (1,)), ((), ())),
        precision=lax.Precision.HIGHEST,
    )
    cells = positions * slot_count
    slot_rows = -(-slot_energy.size // cells)
    energy_rows = -(-events // cells)
    used = events * fold + slot_rows + energy_rows
    spare = -used % (2 * sta_size)
    flat_slot = jnp.pad(slot_energy.reshape(-1), (0, slot_rows * cells - slot_energy.size))
    flat_event = jnp.pad(event_energy, (0, energy_rows * cells - events))
    packed = jnp.concatenate(
        [
            lag_scores,
            flat_slot.reshape(slot_rows, positions, slot_count),
            flat_event.reshape(energy_rows, positions, slot_count),
            jnp.zeros((spare, positions, slot_count), jnp.float32),
        ],
        axis=0,
    )
    total = sta_allreduce(packed)
    base = events * fold
    slot_all = total[base : base + slot_rows].reshape(-1)[: lag_count * slot_count]
    event_all = total[base + slot_rows : base + slot_rows + energy_rows].reshape(-1)[:events]
    scores_all = total[:base].reshape(events, fold, positions, slot_count)
    scores_all = jnp.transpose(scores_all, (0, 2, 1, 3)).reshape(
        events, positions * fold, slot_count
    )[:, :lag_count]
    return normalize(scores_all, slot_all.reshape(lag_count, slot_count), event_all)


def solution(mesh):
    return jax.shard_map(
        body,
        mesh=mesh,
        in_specs=(P("evt", "sta", None), P("sta"), P("evt", None)),
        out_specs=P("evt", None, None),
        check_vma=False,
    )
```

```python
import jax
import jax.numpy as jnp
from jax import lax
from jax.experimental.layout import Layout, with_layout_constraint
from jax.sharding import PartitionSpec as P

WIN = 200
MAXLAG = 40
FOLD = 4


def band_table(extent, lag_count):
    sample = jnp.arange(extent, dtype=jnp.int32)[:, None]
    shift = jnp.arange(lag_count, dtype=jnp.int32)[None, :]
    return ((sample >= shift) & (sample < shift + WIN)).astype(jnp.float32)


def normalize(lag_scores, slot_energy, event_energy):
    return lag_scores / jnp.sqrt(event_energy[:, None, None] * slot_energy[None, :, :] + 1e-06)


def exchange(value, axis, bit, size):
    return lax.ppermute(value, axis, [(i, i ^ bit) for i in range(size)])


def pick(pair, upper):
    return jnp.where(upper, pair[1], pair[0]), jnp.where(upper, pair[0], pair[1])


def place(mine, other, upper):
    return jnp.where(upper, jnp.stack([other, mine]), jnp.stack([mine, other]))


def sta_allreduce(data):
    axis = "sta"
    size = lax.axis_size(axis)
    if size & (size - 1) or size == 1:
        return lax.psum(data, axis)
    index = lax.axis_index(axis)
    bits = [1 << k for k in range(size.bit_length() - 1)]
    orders = [bits, bits[::-1]]
    half = data.shape[0] // 2
    accs = [data[:half], data[half:]]
    for stage in range(len(bits)):
        sends, keeps = [], []
        for h in range(2):
            bit = orders[h][stage]
            acc = accs[h].reshape((2, accs[h].shape[0] // 2) + accs[h].shape[1:])
            keep, send = pick(acc, (index & bit) != 0)
            sends.append(send)
            keeps.append(keep)
        sends = lax.optimization_barrier(sends)
        got = [exchange(sends[h], axis, orders[h][stage], size) for h in range(2)]
        got = lax.optimization_barrier(got)
        accs = [keeps[h] + got[h] for h in range(2)]
    for stage in reversed(range(len(bits))):
        accs = lax.optimization_barrier(accs)
        got = [exchange(accs[h], axis, orders[h][stage], size) for h in range(2)]
        got = lax.optimization_barrier(got)
        accs = [
            place(accs[h], got[h], (index & orders[h][stage]) != 0).reshape(
                (-1,) + accs[h].shape[1:]
            )
            for h in range(2)
        ]
    return jnp.concatenate(accs, axis=0)


def body(traces, channel_valid, partner_block):
    events, channels, extent = traces.shape
    partners = partner_block.shape[1]
    devices_evt = lax.axis_size("evt")
    sta_size = lax.axis_size("sta")
    capacity = max(2, (events * partners + devices_evt - 1) // devices_evt)
    slot_count = devices_evt * capacity
    lag_count = extent - WIN + 1
    flat = partner_block.reshape(-1)
    owner_hot = (flat[:, None] == jnp.arange(devices_evt, dtype=jnp.int32)[None, :]).astype(
        jnp.int32
    )
    before = jnp.cumsum(owner_hot, axis=0) - owner_hot
    ranking = jnp.sum(before * owner_hot, axis=1)
    target = flat * capacity + ranking
    slot_hot = target[:, None] == jnp.arange(slot_count, dtype=jnp.int32)[None, :]
    row_event = jnp.arange(events * partners, dtype=jnp.int32) // partners
    filled = jnp.any(slot_hot, axis=0)
    source = jnp.sum(jnp.where(slot_hot, row_event[:, None], 0), axis=0)
    padded = jnp.pad(traces, ((0, 1), (0, 0), (0, 0)))
    outgoing = jnp.take(
        padded, jnp.where(filled, source, events), axis=0, mode="clip"
    )
    received = lax.all_to_all(
        outgoing,
        "evt",
        split_axis=0,
        concat_axis=0,
        tiled=True,
    )
    received = with_layout_constraint(received, Layout((2, 1, 0)))
    valid = channel_valid.astype(jnp.bfloat16)
    template = traces[:, :, MAXLAG : MAXLAG + WIN] * valid[None, :, None]
    fold = FOLD
    positions = -(-lag_count // fold)
    span = WIN + fold - 1
    reach = (positions - 1) * fold + span
    shifted = [
        jnp.pad(template, ((0, 0), (0, 0), (d, fold - 1 - d))) for d in range(fold)
    ]
    expanded = jnp.stack(shifted, axis=1).reshape(events * fold, channels, span)
    widened = jnp.pad(received, ((0, 0), (0, 0), (0, max(0, reach - extent))))
    lag_scores = lax.conv_general_dilated(
        widened,
        expanded,
        (fold,),
        "VALID",
        dimension_numbers=("NCH", "OIH", "CHN"),
        preferred_element_type=jnp.float32,
    )
    lag_scores = with_layout_constraint(lag_scores, Layout((1, 0, 2)))
    event_energy = jnp.sum(jnp.square(template.astype(jnp.float32)), axis=(1, 2))
    squares_sum = jnp.sum(
        jnp.square(received.astype(jnp.float32)) * channel_valid.astype(jnp.float32)[None, :, None],
        axis=1,
    )
    slot_energy = lax.dot_general(
        band_table(extent, lag_count),
        squares_sum,
        (((0,), (1,)), ((), ())),
        precision=lax.Precision.HIGHEST,
    )
    cells = positions * slot_count
    slot_rows = -(-slot_energy.size // cells)
    energy_rows = -(-events // cells)
    used = events * fold + slot_rows + energy_rows
    spare = -used % (2 * sta_size)
    flat_slot = jnp.pad(slot_energy.reshape(-1), (0, slot_rows * cells - slot_energy.size))
    flat_event = jnp.pad(event_energy, (0, energy_rows * cells - events))
    packed = jnp.concatenate(
        [
            lag_scores,
            flat_slot.reshape(slot_rows, positions, slot_count),
            flat_event.reshape(energy_rows, positions, slot_count),
            jnp.zeros((spare, positions, slot_count), jnp.float32),
        ],
        axis=0,
    )
    total = sta_allreduce(packed)
    base = events * fold
    slot_all = total[base : base + slot_rows].reshape(-1)[: lag_count * slot_count]
    event_all = total[base + slot_rows : base + slot_rows + energy_rows].reshape(-1)[:events]
    scores_all = total[:base].reshape(events, fold, positions, slot_count)
    scores_all = jnp.transpose(scores_all, (0, 2, 1, 3)).reshape(
        events, positions * fold, slot_count
    )[:, :lag_count]
    return normalize(scores_all, slot_all.reshape(lag_count, slot_count), event_all)


def solution(mesh):
    return jax.shard_map(
        body,
        mesh=mesh,
        in_specs=(P("evt", "sta", None), P("sta"), P("evt", None)),
        out_specs=P("evt", None, None),
        check_vma=False,
    )
```

```python
import jax
import jax.numpy as jnp
from jax import lax
from jax.experimental.layout import Layout, with_layout_constraint
from jax.sharding import PartitionSpec as P

WIN = 200
MAXLAG = 40
FOLD = 4


def band_table(extent, lag_count):
    sample = jnp.arange(extent, dtype=jnp.int32)[:, None]
    shift = jnp.arange(lag_count, dtype=jnp.int32)[None, :]
    return ((sample >= shift) & (sample < shift + WIN)).astype(jnp.float32)


def normalize(lag_scores, slot_energy, event_energy):
    return lag_scores / jnp.sqrt(event_energy[:, None, None] * slot_energy[None, :, :] + 1e-06)


def exchange(value, axis, bit, size):
    return lax.ppermute(value, axis, [(i, i ^ bit) for i in range(size)])


def pick(pair, upper):
    return jnp.where(upper, pair[1], pair[0]), jnp.where(upper, pair[0], pair[1])


def place(mine, other, upper):
    return jnp.where(upper, jnp.stack([other, mine]), jnp.stack([mine, other]))


def sta_allreduce(data):
    axis = "sta"
    size = lax.axis_size(axis)
    if size & (size - 1) or size == 1:
        return lax.psum(data, axis)
    index = lax.axis_index(axis)
    bits = [1 << k for k in range(size.bit_length() - 1)]
    orders = [bits, bits[::-1]]
    half = data.shape[0] // 2
    accs = [data[:half], data[half:]]
    for stage in range(len(bits)):
        sends, keeps = [], []
        for h in range(2):
            bit = orders[h][stage]
            acc = accs[h].reshape((2, accs[h].shape[0] // 2) + accs[h].shape[1:])
            keep, send = pick(acc, (index & bit) != 0)
            sends.append(send)
            keeps.append(keep)
        sends = lax.optimization_barrier(sends)
        got = [exchange(sends[h], axis, orders[h][stage], size) for h in range(2)]
        got = lax.optimization_barrier(got)
        accs = [keeps[h] + got[h] for h in range(2)]
    for stage in reversed(range(len(bits))):
        accs = lax.optimization_barrier(accs)
        got = [exchange(accs[h], axis, orders[h][stage], size) for h in range(2)]
        got = lax.optimization_barrier(got)
        accs = [
            place(accs[h], got[h], (index & orders[h][stage]) != 0).reshape(
                (-1,) + accs[h].shape[1:]
            )
            for h in range(2)
        ]
    return jnp.concatenate(accs, axis=0)


def body(traces, channel_valid, partner_block):
    events, channels, extent = traces.shape
    partners = partner_block.shape[1]
    devices_evt = lax.axis_size("evt")
    sta_size = lax.axis_size("sta")
    capacity = max(2, (events * partners + devices_evt - 1) // devices_evt)
    slot_count = devices_evt * capacity
    lag_count = extent - WIN + 1
    flat = partner_block.reshape(-1)
    owner_hot = (flat[:, None] == jnp.arange(devices_evt, dtype=jnp.int32)[None, :]).astype(
        jnp.int32
    )
    before = jnp.cumsum(owner_hot, axis=0) - owner_hot
    ranking = jnp.sum(before * owner_hot, axis=1)
    target = flat * capacity + ranking
    slot_hot = target[:, None] == jnp.arange(slot_count, dtype=jnp.int32)[None, :]
    row_event = jnp.arange(events * partners, dtype=jnp.int32) // partners
    filled = jnp.any(slot_hot, axis=0)
    source = jnp.sum(jnp.where(slot_hot, row_event[:, None], 0), axis=0)
    padded = jnp.pad(traces, ((0, 1), (0, 0), (0, 0)))
    outgoing = jnp.take(
        padded, jnp.where(filled, source, events), axis=0, mode="clip"
    )
    valid = channel_valid.astype(jnp.bfloat16)
    valid_wide = channel_valid.astype(jnp.float32)
    template = traces[:, :, MAXLAG : MAXLAG + WIN] * valid[None, :, None]
    fold = FOLD
    positions = -(-lag_count // fold)
    span = WIN + fold - 1
    reach = (positions - 1) * fold + span
    shifted = [
        jnp.pad(template, ((0, 0), (0, 0), (d, fold - 1 - d))) for d in range(fold)
    ]
    expanded = jnp.stack(shifted, axis=1).reshape(events * fold, channels, span)
    event_energy = jnp.sum(jnp.square(template.astype(jnp.float32)), axis=(1, 2))
    cut = channels // 2 if channels % 2 == 0 else channels
    bounds = [(0, cut), (cut, channels)] if cut < channels else [(0, channels)]
    lag_scores = None
    squares_sum = None
    received = None
    for low, high in bounds:
        sending = outgoing[:, low:high]
        if received is not None:
            received, sending = lax.optimization_barrier((received, sending))
        received = lax.all_to_all(sending, "evt", split_axis=0, concat_axis=0, tiled=True)
        received = with_layout_constraint(received, Layout((2, 1, 0)))
        widened = jnp.pad(received, ((0, 0), (0, 0), (0, max(0, reach - extent))))
        part = lax.conv_general_dilated(
            widened,
            expanded[:, low:high],
            (fold,),
            "VALID",
            dimension_numbers=("NCH", "OIH", "CHN"),
            preferred_element_type=jnp.float32,
        )
        part = with_layout_constraint(part, Layout((1, 0, 2)))
        squares = jnp.sum(
            jnp.square(received.astype(jnp.float32)) * valid_wide[None, low:high, None], axis=1
        )
        lag_scores = part if lag_scores is None else lag_scores + part
        squares_sum = squares if squares_sum is None else squares_sum + squares
    lag_scores = with_layout_constraint(lag_scores, Layout((1, 0, 2)))
    slot_energy = lax.dot_general(
        band_table(extent, lag_count),
        squares_sum,
        (((0,), (1,)), ((), ())),
        precision=lax.Precision.HIGHEST,
    )
    cells = positions * slot_count
    slot_rows = -(-slot_energy.size // cells)
    energy_rows = -(-events // cells)
    used = events * fold + slot_rows + energy_rows
    spare = -used % (2 * sta_size)
    flat_slot = jnp.pad(slot_energy.reshape(-1), (0, slot_rows * cells - slot_energy.size))
    flat_event = jnp.pad(event_energy, (0, energy_rows * cells - events))
    packed = jnp.concatenate(
        [
            lag_scores,
            flat_slot.reshape(slot_rows, positions, slot_count),
            flat_event.reshape(energy_rows, positions, slot_count),
            jnp.zeros((spare, positions, slot_count), jnp.float32),
        ],
        axis=0,
    )
    total = sta_allreduce(packed)
    base = events * fold
    slot_all = total[base : base + slot_rows].reshape(-1)[: lag_count * slot_count]
    event_all = total[base + slot_rows : base + slot_rows + energy_rows].reshape(-1)[:events]
    scores_all = total[:base].reshape(events, fold, positions, slot_count)
    scores_all = jnp.transpose(scores_all, (0, 2, 1, 3)).reshape(
        events, positions * fold, slot_count
    )[:, :lag_count]
    return normalize(scores_all, slot_all.reshape(lag_count, slot_count), event_all)


def solution(mesh):
    return jax.shard_map(
        body,
        mesh=mesh,
        in_specs=(P("evt", "sta", None), P("sta"), P("evt", None)),
        out_specs=P("evt", None, None),
        check_vma=False,
    )
```

```python
import jax
import jax.numpy as jnp
from jax import lax
from jax.experimental.layout import Layout, with_layout_constraint
from jax.sharding import PartitionSpec as P

WIN = 200
MAXLAG = 40
FOLD = 4


def band_table(extent, lag_count):
    sample = jnp.arange(extent, dtype=jnp.int32)[:, None]
    shift = jnp.arange(lag_count, dtype=jnp.int32)[None, :]
    return ((sample >= shift) & (sample < shift + WIN)).astype(jnp.float32)


def normalize(lag_scores, slot_energy, event_energy):
    return lag_scores / jnp.sqrt(event_energy[:, None, None] * slot_energy[None, :, :] + 1e-06)


def exchange(value, axis, bit, size):
    return lax.ppermute(value, axis, [(i, i ^ bit) for i in range(size)])


def pick(pair, upper):
    return jnp.where(upper, pair[1], pair[0]), jnp.where(upper, pair[0], pair[1])


def place(mine, other, upper):
    return jnp.where(upper, jnp.stack([other, mine]), jnp.stack([mine, other]))


def sta_allreduce(data):
    axis = "sta"
    size = lax.axis_size(axis)
    if size & (size - 1) or size == 1:
        return lax.psum(data, axis)
    index = lax.axis_index(axis)
    bits = [1 << k for k in range(size.bit_length() - 1)]
    orders = [bits, bits[::-1]]
    half = data.shape[0] // 2
    accs = [data[:half], data[half:]]
    for stage in range(len(bits)):
        sends, keeps = [], []
        for h in range(2):
            bit = orders[h][stage]
            acc = accs[h].reshape((2, accs[h].shape[0] // 2) + accs[h].shape[1:])
            keep, send = pick(acc, (index & bit) != 0)
            sends.append(send)
            keeps.append(keep)
        sends = lax.optimization_barrier(sends)
        got = [exchange(sends[h], axis, orders[h][stage], size) for h in range(2)]
        got = lax.optimization_barrier(got)
        accs = [keeps[h] + got[h] for h in range(2)]
    for stage in reversed(range(len(bits))):
        accs = lax.optimization_barrier(accs)
        got = [exchange(accs[h], axis, orders[h][stage], size) for h in range(2)]
        got = lax.optimization_barrier(got)
        accs = [
            place(accs[h], got[h], (index & orders[h][stage]) != 0).reshape(
                (-1,) + accs[h].shape[1:]
            )
            for h in range(2)
        ]
    return jnp.concatenate(accs, axis=0)


def body(traces, channel_valid, partner_block):
    events, channels, extent = traces.shape
    partners = partner_block.shape[1]
    devices_evt = lax.axis_size("evt")
    sta_size = lax.axis_size("sta")
    capacity = max(2, (events * partners + devices_evt - 1) // devices_evt)
    slot_count = devices_evt * capacity
    lag_count = extent - WIN + 1
    flat = partner_block.reshape(-1)
    owner_hot = (flat[:, None] == jnp.arange(devices_evt, dtype=jnp.int32)[None, :]).astype(
        jnp.int32
    )
    before = jnp.cumsum(owner_hot, axis=0) - owner_hot
    ranking = jnp.sum(before * owner_hot, axis=1)
    target = flat * capacity + ranking
    slot_hot = target[:, None] == jnp.arange(slot_count, dtype=jnp.int32)[None, :]
    row_event = jnp.arange(events * partners, dtype=jnp.int32) // partners
    filled = jnp.any(slot_hot, axis=0)
    source = jnp.sum(jnp.where(slot_hot, row_event[:, None], 0), axis=0)
    evt_index = lax.axis_index("evt")
    order = jnp.arange(devices_evt, dtype=jnp.int32) ^ evt_index
    picks = jnp.where(filled, source, events).reshape(devices_evt, capacity)
    picks = jnp.take(picks, order, axis=0, mode="clip").reshape(-1)
    padded = jnp.pad(traces, ((0, 1), (0, 0), (0, 0)))
    outgoing = jnp.take(padded, picks, axis=0, mode="clip").reshape(
        devices_evt, capacity, channels, extent
    )
    got = [outgoing[0]] + [
        lax.ppermute(outgoing[k], "evt", [(i, i ^ k) for i in range(devices_evt)])
        for k in range(1, devices_evt)
    ]
    received = jnp.take(jnp.stack(got), order, axis=0, mode="clip").reshape(
        slot_count, channels, extent
    )
    received = with_layout_constraint(received, Layout((2, 1, 0)))
    valid = channel_valid.astype(jnp.bfloat16)
    template = traces[:, :, MAXLAG : MAXLAG + WIN] * valid[None, :, None]
    fold = FOLD
    positions = -(-lag_count // fold)
    span = WIN + fold - 1
    reach = (positions - 1) * fold + span
    shifted = [
        jnp.pad(template, ((0, 0), (0, 0), (d, fold - 1 - d))) for d in range(fold)
    ]
    expanded = jnp.stack(shifted, axis=1).reshape(events * fold, channels, span)
    widened = jnp.pad(received, ((0, 0), (0, 0), (0, max(0, reach - extent))))
    lag_scores = lax.conv_general_dilated(
        widened,
        expanded,
        (fold,),
        "VALID",
        dimension_numbers=("NCH", "OIH", "CHN"),
        preferred_element_type=jnp.float32,
    )
    lag_scores = with_layout_constraint(lag_scores, Layout((1, 0, 2)))
    event_energy = jnp.sum(jnp.square(template.astype(jnp.float32)), axis=(1, 2))
    squares_sum = jnp.sum(
        jnp.square(received.astype(jnp.float32)) * channel_valid.astype(jnp.float32)[None, :, None],
        axis=1,
    )
    slot_energy = lax.dot_general(
        band_table(extent, lag_count),
        squares_sum,
        (((0,), (1,)), ((), ())),
        precision=lax.Precision.HIGHEST,
    )
    cells = positions * slot_count
    slot_rows = -(-slot_energy.size // cells)
    energy_rows = -(-events // cells)
    used = events * fold + slot_rows + energy_rows
    spare = -used % (2 * sta_size)
    flat_slot = jnp.pad(slot_energy.reshape(-1), (0, slot_rows * cells - slot_energy.size))
    flat_event = jnp.pad(event_energy, (0, energy_rows * cells - events))
    packed = jnp.concatenate(
        [
            lag_scores,
            flat_slot.reshape(slot_rows, positions, slot_count),
            flat_event.reshape(energy_rows, positions, slot_count),
            jnp.zeros((spare, positions, slot_count), jnp.float32),
        ],
        axis=0,
    )
    total = sta_allreduce(packed)
    base = events * fold
    slot_all = total[base : base + slot_rows].reshape(-1)[: lag_count * slot_count]
    event_all = total[base + slot_rows : base + slot_rows + energy_rows].reshape(-1)[:events]
    scores_all = total[:base].reshape(events, fold, positions, slot_count)
    scores_all = jnp.transpose(scores_all, (0, 2, 1, 3)).reshape(
        events, positions * fold, slot_count
    )[:, :lag_count]
    return normalize(scores_all, slot_all.reshape(lag_count, slot_count), event_all)


def solution(mesh):
    return jax.shard_map(
        body,
        mesh=mesh,
        in_specs=(P("evt", "sta", None), P("sta"), P("evt", None)),
        out_specs=P("evt", None, None),
        check_vma=False,
    )
```

```python
import jax
import jax.numpy as jnp
from jax import lax
from jax.experimental.layout import Layout, with_layout_constraint
from jax.sharding import PartitionSpec as P

WIN = 200
MAXLAG = 40
FOLD = 4


def band_table(extent, lag_count):
    sample = jnp.arange(extent, dtype=jnp.int32)[:, None]
    shift = jnp.arange(lag_count, dtype=jnp.int32)[None, :]
    return ((sample >= shift) & (sample < shift + WIN)).astype(jnp.float32)


def normalize(lag_scores, slot_energy, event_energy):
    return lag_scores / jnp.sqrt(event_energy[:, None, None] * slot_energy[None, :, :] + 1e-06)


def exchange(value, axis, bit, size):
    return lax.ppermute(value, axis, [(i, i ^ bit) for i in range(size)])


def pick(pair, upper):
    return jnp.where(upper, pair[1], pair[0]), jnp.where(upper, pair[0], pair[1])


def place(mine, other, upper):
    return jnp.where(upper, jnp.stack([other, mine]), jnp.stack([mine, other]))


def sta_allreduce(data):
    axis = "sta"
    size = lax.axis_size(axis)
    if size & (size - 1) or size == 1:
        return lax.psum(data, axis)
    index = lax.axis_index(axis)
    bits = [1 << k for k in range(size.bit_length() - 1)]
    orders = [bits, bits[::-1]]
    half = data.shape[0] // 2
    accs = [data[:half], data[half:]]
    for stage in range(len(bits)):
        sends, keeps = [], []
        for h in range(2):
            bit = orders[h][stage]
            acc = accs[h].reshape((2, accs[h].shape[0] // 2) + accs[h].shape[1:])
            keep, send = pick(acc, (index & bit) != 0)
            sends.append(send)
            keeps.append(keep)
        sends = lax.optimization_barrier(sends)
        got = [exchange(sends[h], axis, orders[h][stage], size) for h in range(2)]
        got = lax.optimization_barrier(got)
        accs = [keeps[h] + got[h] for h in range(2)]
    for stage in reversed(range(len(bits))):
        accs = lax.optimization_barrier(accs)
        got = [exchange(accs[h], axis, orders[h][stage], size) for h in range(2)]
        got = lax.optimization_barrier(got)
        accs = [
            place(accs[h], got[h], (index & orders[h][stage]) != 0).reshape(
                (-1,) + accs[h].shape[1:]
            )
            for h in range(2)
        ]
    return jnp.concatenate(accs, axis=0)


def body(traces, channel_valid, partner_block):
    events, channels, extent = traces.shape
    partners = partner_block.shape[1]
    devices_evt = lax.axis_size("evt")
    sta_size = lax.axis_size("sta")
    capacity = max(2, (events * partners + devices_evt - 1) // devices_evt)
    slot_count = devices_evt * capacity
    lag_count = extent - WIN + 1
    flat = partner_block.reshape(-1)
    owner_hot = (flat[:, None] == jnp.arange(devices_evt, dtype=jnp.int32)[None, :]).astype(
        jnp.int32
    )
    before = jnp.cumsum(owner_hot, axis=0) - owner_hot
    ranking = jnp.sum(before * owner_hot, axis=1)
    target = flat * capacity + ranking
    slot_hot = target[:, None] == jnp.arange(slot_count, dtype=jnp.int32)[None, :]
    row_event = jnp.arange(events * partners, dtype=jnp.int32) // partners
    filled = jnp.any(slot_hot, axis=0)
    source = jnp.sum(jnp.where(slot_hot, row_event[:, None], 0), axis=0)
    padded = jnp.pad(traces, ((0, 1), (0, 0), (0, 0)))
    outgoing = jnp.take(
        padded, jnp.where(filled, source, events), axis=0, mode="clip"
    )
    received = lax.all_to_all(
        outgoing,
        "evt",
        split_axis=0,
        concat_axis=0,
        tiled=True,
    )
    received = with_layout_constraint(received, Layout((2, 1, 0)))
    valid = channel_valid.astype(jnp.bfloat16)
    template = traces[:, :, MAXLAG : MAXLAG + WIN] * valid[None, :, None]
    fold = FOLD
    positions = -(-lag_count // fold)
    span = WIN + fold - 1
    reach = (positions - 1) * fold + span
    shifted = [
        jnp.pad(template, ((0, 0), (0, 0), (d, fold - 1 - d))) for d in range(fold)
    ]
    expanded = jnp.stack(shifted, axis=1).reshape(events * fold, channels, span)
    widened = jnp.pad(received, ((0, 0), (0, 0), (0, max(0, reach - extent))))
    lag_scores = lax.conv_general_dilated(
        widened,
        expanded,
        (fold,),
        "VALID",
        dimension_numbers=("NCH", "OIH", "CHN"),
        preferred_element_type=jnp.float32,
    )
    lag_scores = with_layout_constraint(lag_scores, Layout((1, 0, 2)))
    event_energy = jnp.sum(jnp.square(template.astype(jnp.float32)), axis=(1, 2))
    squares_sum = jnp.sum(
        jnp.square(received.astype(jnp.float32)) * channel_valid.astype(jnp.float32)[None, :, None],
        axis=1,
    )
    slot_energy = lax.dot_general(
        band_table(extent, lag_count),
        squares_sum,
        (((0,), (1,)), ((), ())),
        precision=lax.Precision.HIGHEST,
    )
    waste = positions * fold - lag_count
    room = events * waste * slot_count
    needed = slot_energy.size + events
    base = events * fold
    if waste and room >= needed and base % (4 * sta_size) == 0:
        stash = jnp.pad(
            jnp.concatenate([slot_energy.reshape(-1), event_energy]), (0, room - needed)
        ).reshape(events, waste, slot_count)
        grid = lag_scores.reshape(events, fold, positions, slot_count)
        grid = grid.at[:, fold - waste :, positions - 1, :].set(stash)
        packed = with_layout_constraint(grid.reshape(base, positions, slot_count), Layout((1, 0, 2)))
        total = sta_allreduce(packed).reshape(events, fold, positions, slot_count)
        spilled = total[:, fold - waste :, positions - 1, :].reshape(-1)
        slot_all = spilled[: slot_energy.size]
        event_all = spilled[slot_energy.size : needed]
        scores_all = total
    else:
        cells = positions * slot_count
        slot_rows = -(-slot_energy.size // cells)
        energy_rows = -(-events // cells)
        spare = -(base + slot_rows + energy_rows) % (2 * sta_size)
        flat_slot = jnp.pad(slot_energy.reshape(-1), (0, slot_rows * cells - slot_energy.size))
        flat_event = jnp.pad(event_energy, (0, energy_rows * cells - events))
        packed = jnp.concatenate(
            [
                lag_scores,
                flat_slot.reshape(slot_rows, positions, slot_count),
                flat_event.reshape(energy_rows, positions, slot_count),
                jnp.zeros((spare, positions, slot_count), jnp.float32),
            ],
            axis=0,
        )
        total = sta_allreduce(packed)
        slot_all = total[base : base + slot_rows].reshape(-1)[: slot_energy.size]
        event_all = total[base + slot_rows : base + slot_rows + energy_rows].reshape(-1)[:events]
        scores_all = total[:base].reshape(events, fold, positions, slot_count)
    scores_all = jnp.transpose(scores_all, (0, 2, 1, 3)).reshape(
        events, positions * fold, slot_count
    )[:, :lag_count]
    return normalize(scores_all, slot_all.reshape(lag_count, slot_count), event_all)


def solution(mesh):
    return jax.shard_map(
        body,
        mesh=mesh,
        in_specs=(P("evt", "sta", None), P("sta"), P("evt", None)),
        out_specs=P("evt", None, None),
        check_vma=False,
    )
```
